512 devices in a mesh: req: 128 (over x, z, core), head: 4 (over y).
Axes of the slice: x: 4, y: 4, z: 16, core: 2. Of those that a mesh axis runs over, the one named last changes fastest.
Arguments:
- queries: bfloat16 [128, 16, 2048], P('req', None, 'head'), may hold values from -6 to 6
- forget_logits: bfloat16 [128, 16, 2048], P('req', None, 'head'), may hold values from -8 to 8
- values: bfloat16 [128, 16, 2048], P('req', None, 'head'), may hold values from -6 to 6
- gate_input: bfloat16 [128, 16, 2048], P('req', None, 'head'), may hold values from -6 to 6
- init_states: float32 [128, 16, 128, 128], P('req', 'head'), may hold values from -4 to 4
- norm_gain: float32 [128], replicated, may hold values from 0.1 to 1.9
- out_weight: bfloat16 [2048, 2048], P('head'), may hold values from -0.125 to 0.125
- dealing: int32 [128], P('req'), may hold values from 0 to 127, as said below
- accepted: int32 [128], P('req'), may hold values from 0 to 16, as said below
Outputs:
- verified: bfloat16 [128, 16, 2048], P('req', None, 'head')
- new_states: float32 [128, 16, 128, 128], P('req', 'head')
The draws below stay inside these ranges and needn't reach their ends.
Inputs may be any that keep to these rules, and one draw needn't show every extreme that they name: `dealing`: each request appears in exactly one dealt slot. `accepted`: some request accepts all 16 draft tokens and some accepts none.
All inputs are finite; a program needn't handle non-finite values.
Results may differ from the reference program's by a relative error of at most 0.0049.
Values may be sent and summed in bfloat16 or wider, within the bound.
No kernel may reach another device: no remote copies, remote signals or barrier semaphores. Data moves between devices by JAX's collectives and lax.ppermute only.
A program may use at most 64 MiB of HBM per device.

```python
import jax
import jax.numpy as jnp
from jax import lax

HEADS = 16
HEAD_DIM = 128
D = 2048
DRAFT = 16
REQS = 128


def draw_dealing(key, part):
    shuffled = jax.random.permutation(jax.random.fold_in(key, 11), REQS).astype(jnp.int32)
    middle = REQS // 2
    where_middle = jnp.argmax(shuffled == middle)
    first_entry = shuffled[0]
    shuffled = shuffled.at[where_middle].set(first_entry).at[0].set(middle)
    return shuffled.astype(jnp.int32)


def draw_accepted(key, part):
    first_key, second_key = jax.random.split(jax.random.fold_in(key, 7))
    counts = jax.random.randint(first_key, (REQS,), 0, DRAFT + 1)
    shuffled = jax.random.permutation(second_key, REQS)
    counts = counts.at[shuffled[0]].set(DRAFT).at[shuffled[1]].set(0)
    return counts.astype(jnp.int32)


def levels(key, dims, cuts, low, top_value):
    factor_of = 1.0
    for position, parts in cuts:
        heights = jax.random.uniform(jax.random.fold_in(jax.random.fold_in(key, 6), position), (parts,), jnp.float32, low / len(cuts), top_value / len(cuts))
        factor_of = factor_of * jnp.repeat(jnp.exp(heights), dims[position] // parts).reshape((-1,) + (1,) * (len(dims) - 1 - position))
    return factor_of


def noise(key, dims, width, bound, shards=(), kind=jnp.bfloat16):
    entries = jax.random.normal(key, dims, jnp.float32) * width
    if len(shards) > 0:
        entries = levels(key, dims, shards, -0.22, 0.18) * entries
    return jnp.clip(entries, min=-bound, max=bound).astype(kind)


def setup_inputs(seed: int = 0) -> dict:
    streams_of = jax.random.split(jax.random.key(seed), 10)
    return {
        "queries": noise(streams_of[0], (REQS, DRAFT, D), 1.0, 6.0, ((0, 128), (2, 4))),
        "forget_logits": noise(streams_of[1], (REQS, DRAFT, D), 2.0, 8.0, ((0, 128), (2, 4))),
        "values": noise(streams_of[2], (REQS, DRAFT, D), 1.0, 6.0, ((0, 128), (2, 4))),
        "gate_input": noise(streams_of[3], (REQS, DRAFT, D), 1.0, 6.0, ((0, 128), (2, 4))),
        "init_states": noise(streams_of[4], (REQS, HEADS, HEAD_DIM, HEAD_DIM), 0.5, 4.0, ((0, 128), (1, 4)), jnp.float32),
        "norm_gain": jnp.clip(1.0 + 0.18 * jax.random.normal(streams_of[5], (HEAD_DIM,), jnp.float32), 0.1, 1.9),
        "out_weight": noise(streams_of[6], (D, D), D ** -0.5, 0.125, ((0, 4),)),
        "dealing": draw_dealing(jax.random.fold_in(streams_of[9], 71), 0),
        "accepted": draw_accepted(jax.random.fold_in(streams_of[9], 71), 0),
    }


lower_bound = 0.8
norm_eps = 1e-05

def reference(queries, forget_logits, values, gate_input, init_states, norm_gain, out_weight, dealing, accepted):
    request_total = dealing.shape[0]
    inverse = jnp.zeros((request_total,), jnp.int32).at[dealing].set(jnp.arange(request_total, dtype=jnp.int32))
    tokens_q = queries[inverse]
    tokens_f = forget_logits[inverse]
    tokens_v = values[inverse]
    tokens_g = gate_input[inverse]

    def heads_of(tensor):
        return jnp.moveaxis(tensor.astype(jnp.float32).reshape(request_total, DRAFT, HEADS, HEAD_DIM), 1, 0)
    query_seq = heads_of(tokens_q)
    forget_seq = lower_bound + (1.0 - lower_bound) * jax.nn.sigmoid(heads_of(tokens_f))
    value_seq = heads_of(tokens_v)
    numbers = jnp.arange(1, DRAFT + 1, dtype=jnp.int32)

    def advance(state_pair, inputs):
        current, chosen = state_pair
        query_now, forget_now, value_now, number = inputs
        current = forget_now[..., None] * current + (1.0 - forget_now)[..., None] * value_now[..., None, :]
        chosen = jnp.where((accepted == number)[:, None, None, None], current, chosen)
        output = jnp.einsum('rhk,rhkv->rhv', query_now, current, precision=lax.Precision.HIGHEST)
        return ((current, chosen), output)
    (last_state, chosen), outputs = lax.scan(advance, (init_states, init_states), (query_seq, forget_seq, value_seq, numbers))
    outputs = jnp.moveaxis(outputs, 0, 1)
    meansq = lax.optimization_barrier(jnp.mean(outputs * outputs, axis=-1, keepdims=True))
    gate_heads = tokens_g.astype(jnp.float32).reshape(request_total, DRAFT, HEADS, HEAD_DIM)
    mixed_rows = (outputs * lax.rsqrt(meansq + norm_eps) * norm_gain * jax.nn.silu(gate_heads)).astype(jnp.bfloat16)
    mixed_rows = mixed_rows.reshape(request_total * DRAFT, HEADS * HEAD_DIM)
    verified = jnp.dot(mixed_rows, out_weight, preferred_element_type=jnp.float32).astype(jnp.bfloat16)
    verified = verified.reshape(request_total, DRAFT, HEADS * HEAD_DIM)
    return (verified, chosen)
```

```python
import jax
import jax.numpy as jnp
from jax import lax
from jax.sharding import Mesh, PartitionSpec as P

lower_bound = 0.8
norm_eps = 1e-05

ROW = ("x", "c")
REQ = ("x", "z", "c")


def route_two_stage(token_tuple, dealing):
    rows = jnp.concatenate([t[0] for t in token_tuple], axis=0)
    width = rows.shape[1]
    dest_row = jnp.broadcast_to(dealing.astype(jnp.bfloat16).reshape(1, 1), (1, width))
    payload = jnp.concatenate([rows, dest_row], axis=0)
    gathered = lax.all_gather(payload, ROW, axis=0, tiled=False)
    dest = gathered[:, -1, 0].astype(jnp.int32)
    body = gathered[:, :-1, :]
    zn = lax.axis_size("z")
    my_x = lax.axis_index("x")
    my_c = lax.axis_index("c")
    cn = lax.axis_size("c")
    target = (my_x * zn + jnp.arange(zn, dtype=jnp.int32)) * cn + my_c
    match = (target[:, None] == dest[None, :]).astype(jnp.bfloat16)
    send = jnp.einsum("zk,kre->zre", match, body, preferred_element_type=jnp.float32).astype(jnp.bfloat16)
    got = lax.all_to_all(send, "z", 0, 0, tiled=False)
    mine = jnp.sum(got.astype(jnp.float32), axis=0).astype(jnp.bfloat16)
    n = len(token_tuple)
    per = mine.shape[0] // n
    return tuple(mine[i * per:(i + 1) * per][None] for i in range(n))


def per_device(
    queries,
    forget_logits,
    values,
    gate_input,
    init_states,
    norm_gain,
    out_weight,
    dealing,
    accepted,
):
    local_count = queries.shape[0]
    draft_len = queries.shape[1]
    head_local = init_states.shape[1]
    head_size = init_states.shape[3]
    token_tuple = (queries, forget_logits, values, gate_input)
    tokens_q, tokens_f, tokens_v, tokens_g = route_two_stage(token_tuple, dealing)

    def heads_of(tensor):
        return jnp.moveaxis(
            tensor.astype(jnp.float32).reshape(local_count, draft_len, head_local, head_size), 1, 0
        )

    query_seq = heads_of(tokens_q)
    forget_seq = lower_bound + (1.0 - lower_bound) * jax.nn.sigmoid(heads_of(tokens_f))
    value_seq = heads_of(tokens_v)
    numbers = jnp.arange(1, draft_len + 1, dtype=jnp.int32)

    def advance(state_pair, inputs):
        current, chosen = state_pair
        query_now, forget_now, value_now, number = inputs
        current = (
            forget_now[..., None] * current
            + (1.0 - forget_now)[..., None] * value_now[..., None, :]
        )
        chosen = jnp.where((accepted == number)[:, None, None, None], current, chosen)
        output = jnp.einsum("rhk,rhkv->rhv", query_now, current, precision=lax.Precision.HIGHEST)
        return ((current, chosen), output)

    (last_state, new_states), outputs = lax.scan(
        advance, (init_states, init_states), (query_seq, forget_seq, value_seq, numbers)
    )
    outputs = jnp.moveaxis(outputs, 0, 1)
    meansq = jnp.mean(outputs * outputs, axis=-1, keepdims=True)
    gate_heads = tokens_g.astype(jnp.float32).reshape(local_count, draft_len, head_local, head_size)
    mixed_rows = (
        outputs * lax.rsqrt(meansq + norm_eps) * norm_gain * jax.nn.silu(gate_heads)
    ).astype(jnp.bfloat16)
    mixed_rows = mixed_rows.reshape(local_count * draft_len, head_local * head_size)
    partial_out = jnp.dot(mixed_rows, out_weight, preferred_element_type=jnp.float32)
    hn = lax.axis_size("head")
    rows = partial_out.shape[0]
    split = partial_out.reshape(rows, hn, partial_out.shape[1] // hn)
    swapped = lax.all_to_all(split, "head", 1, 1, tiled=True)
    summed = jnp.sum(swapped, axis=1)
    verified = summed.astype(jnp.bfloat16).reshape(local_count, draft_len, summed.shape[1])
    return (verified, new_states)


def solution(mesh):
    xs, zs, cs = 4, mesh.shape["req"] // 8, 2
    sub = Mesh(mesh.devices.reshape(xs, zs, cs, mesh.shape["head"]), ("x", "z", "c", "head"))
    placed = (
        P(REQ, None, "head"),
        P(REQ, None, "head"),
        P(REQ, None, "head"),
        P(REQ, None, "head"),
        P(REQ, "head", None, None),
        P(),
        P("head", None),
        P(REQ),
        P(REQ),
    )
    return jax.shard_map(
        per_device,
        mesh=sub,
        in_specs=placed,
        out_specs=(P(REQ, None, "head"), P(REQ, "head", None, None)),
        check_vma=False,
    )
```

```python
import jax
import jax.numpy as jnp
from jax import lax
from jax.experimental import pallas as pl
from jax.experimental.pallas import tpu as pltpu
from jax.sharding import Mesh, PartitionSpec as P

lower_bound = 0.8
norm_eps = 1e-05

ROW = ("x", "c")
REQ = ("x", "z", "c")


HI = lax.Precision.HIGHEST


def _dot(a, b):
    return jnp.dot(a, b, precision=HI, preferred_element_type=jnp.float32)


def mixer_kernel(acc_ref, tok_ref, s0_ref, gain_ref, new_ref, mixed_ref):
    acc = acc_ref[0]
    tok = tok_ref[...].astype(jnp.float32)
    t_len = tok.shape[0] // 4
    heads = s0_ref.shape[0]
    hd = s0_ref.shape[2]
    q = tok[0:t_len]
    fl = tok[t_len:2 * t_len]
    v = tok[2 * t_len:3 * t_len]
    g = tok[3 * t_len:4 * t_len]
    a = lower_bound + (1.0 - lower_bound) * (1.0 / (1.0 + jnp.exp(-fl)))
    b = 1.0 - a
    la = jnp.log(a)
    row = lax.broadcasted_iota(jnp.int32, (t_len, t_len), 0)
    col = lax.broadcasted_iota(jnp.int32, (t_len, t_len), 1)
    causal = (col <= row).astype(jnp.float32)
    lc = _dot(causal, la)
    big_a = jnp.exp(lc)
    inv_a = jnp.exp(-lc)
    qa = q * big_a
    ba = b * inv_a
    kept = (lax.broadcasted_iota(jnp.int32, la.shape, 0) < acc).astype(jnp.float32)
    a_acc = jnp.exp(jnp.sum(kept * la, axis=0, keepdims=True))
    w = kept * a_acc * ba
    eye_r = lax.broadcasted_iota(jnp.int32, (hd, hd), 0)
    eye_c = lax.broadcasted_iota(jnp.int32, (hd, hd), 1)
    eye = (eye_r == eye_c).astype(jnp.float32)
    gain = gain_ref[...]
    silu_g = g * (1.0 / (1.0 + jnp.exp(-g)))
    for h in range(heads):
        lanes = slice(h * hd, (h + 1) * hd)
        s0 = s0_ref[h]
        v_h = v[:, lanes]
        qa_h = qa[:, lanes]
        scores = lax.dot_general(qa_h, ba[:, lanes], (((1,), (1,)), ((), ())),
                                 precision=HI, preferred_element_type=jnp.float32)
        o_h = _dot(qa_h, s0) + _dot(scores * causal, v_h)
        diag = eye * a_acc[:, lanes]
        new_ref[h] = _dot(diag, s0) + _dot(jnp.transpose(w[:, lanes]), v_h)
        meansq = jnp.mean(o_h * o_h, axis=-1, keepdims=True)
        mixed = o_h * lax.rsqrt(meansq + norm_eps) * gain * silu_g[:, lanes]
        mixed_ref[:, lanes] = mixed.astype(mixed_ref.dtype)


def mixer(acc, tok, s0, gain):
    heads, hd = s0.shape[0], s0.shape[2]
    t_len = tok.shape[0] // 4
    vmem = pl.BlockSpec(memory_space=pltpu.VMEM)
    return pl.pallas_call(
        mixer_kernel,
        out_shape=(jax.ShapeDtypeStruct(s0.shape, jnp.float32),
                   jax.ShapeDtypeStruct((t_len, heads * hd), jnp.bfloat16)),
        in_specs=[pl.BlockSpec(memory_space=pltpu.SMEM), vmem, vmem, vmem],
        out_specs=(vmem, vmem),
    )(acc, tok, s0, gain)


def route_two_stage(token_tuple, dealing):
    rows = jnp.concatenate([t[0] for t in token_tuple], axis=0)
    width = rows.shape[1]
    dest_row = jnp.broadcast_to(dealing.astype(jnp.bfloat16).reshape(1, 1), (1, width))
    payload = jnp.concatenate([rows, dest_row], axis=0)
    gathered = lax.all_gather(payload, ROW, axis=0, tiled=False)
    dest = gathered[:, -1, 0].astype(jnp.int32)
    body = gathered[:, :-1, :]
    zn = lax.axis_size("z")
    my_x = lax.axis_index("x")
    my_c = lax.axis_index("c")
    cn = lax.axis_size("c")
    target = (my_x * zn + jnp.arange(zn, dtype=jnp.int32)) * cn + my_c
    match = (target[:, None] == dest[None, :]).astype(jnp.bfloat16)
    send = jnp.einsum("zk,kre->zre", match, body, preferred_element_type=jnp.float32).astype(jnp.bfloat16)
    got = lax.all_to_all(send, "z", 0, 0, tiled=False)
    mine = jnp.sum(got.astype(jnp.float32), axis=0).astype(jnp.bfloat16)
    return mine


def per_device(
    queries,
    forget_logits,
    values,
    gate_input,
    init_states,
    norm_gain,
    out_weight,
    dealing,
    accepted,
):
    local_count = queries.shape[0]
    draft_len = queries.shape[1]
    head_local = init_states.shape[1]
    head_size = init_states.shape[3]
    token_tuple = (queries, forget_logits, values, gate_input)
    mine = route_two_stage(token_tuple, dealing)
    new_states, mixed_rows = mixer(accepted, mine, init_states[0], norm_gain.reshape(1, head_size))
    new_states = new_states[None]

    mixed_rows = mixed_rows.reshape(local_count * draft_len, head_local * head_size)
    partial_out = jnp.dot(mixed_rows, out_weight, preferred_element_type=jnp.float32)
    hn = lax.axis_size("head")
    rows = partial_out.shape[0]
    split = partial_out.reshape(rows, hn, partial_out.shape[1] // hn)
    swapped = lax.all_to_all(split, "head", 1, 1, tiled=True)
    summed = jnp.sum(swapped, axis=1)
    verified = summed.astype(jnp.bfloat16).reshape(local_count, draft_len, summed.shape[1])
    return (verified, new_states)


def solution(mesh):
    xs, zs, cs = 4, mesh.shape["req"] // 8, 2
    sub = Mesh(mesh.devices.reshape(xs, zs, cs, mesh.shape["head"]), ("x", "z", "c", "head"))
    placed = (
        P(REQ, None, "head"),
        P(REQ, None, "head"),
        P(REQ, None, "head"),
        P(REQ, None, "head"),
        P(REQ, "head", None, None),
        P(),
        P("head", None),
        P(REQ),
        P(REQ),
    )
    return jax.shard_map(
        per_device,
        mesh=sub,
        in_specs=placed,
        out_specs=(P(REQ, None, "head"), P(REQ, "head", None, None)),
        check_vma=False,
    )
```

```python
import jax
import jax.numpy as jnp
from jax import lax
from jax.experimental import pallas as pl
from jax.experimental.pallas import tpu as pltpu
from jax.sharding import Mesh, PartitionSpec as P

lower_bound = 0.8
norm_eps = 1e-05

ROW = ("x", "c")
REQ = ("x", "z", "c")


HI = lax.Precision.HIGHEST


def _dot(a, b):
    return jnp.dot(a, b, precision=HI, preferred_element_type=jnp.float32)


def mixer_kernel(acc_ref, tok_ref, s0_ref, gain_ref, new_ref, mixed_ref):
    acc = acc_ref[0]
    tok = tok_ref[...].astype(jnp.float32)
    t_len = tok.shape[0] // 4
    heads = s0_ref.shape[0]
    hd = s0_ref.shape[2]
    q = tok[0:t_len]
    fl = tok[t_len:2 * t_len]
    v = tok[2 * t_len:3 * t_len]
    g = tok[3 * t_len:4 * t_len]
    a = lower_bound + (1.0 - lower_bound) * (1.0 / (1.0 + jnp.exp(-fl)))
    b = 1.0 - a
    la = jnp.log(a)
    row = lax.broadcasted_iota(jnp.int32, (t_len, t_len), 0)
    col = lax.broadcasted_iota(jnp.int32, (t_len, t_len), 1)
    causal = (col <= row).astype(jnp.float32)
    lc = _dot(causal, la)
    big_a = jnp.exp(lc)
    inv_a = jnp.exp(-lc)
    qa = q * big_a
    ba = b * inv_a
    kept = (lax.broadcasted_iota(jnp.int32, la.shape, 0) < acc).astype(jnp.float32)
    a_acc = jnp.exp(jnp.sum(kept * la, axis=0, keepdims=True))
    w = kept * a_acc * ba
    eye_r = lax.broadcasted_iota(jnp.int32, (hd, hd), 0)
    eye_c = lax.broadcasted_iota(jnp.int32, (hd, hd), 1)
    eye = (eye_r == eye_c).astype(jnp.float32)
    gain = gain_ref[...]
    silu_g = g * (1.0 / (1.0 + jnp.exp(-g)))
    for h in range(heads):
        lanes = slice(h * hd, (h + 1) * hd)
        s0 = s0_ref[h]
        v_h = v[:, lanes]
        qa_h = qa[:, lanes]
        scores = lax.dot_general(qa_h, ba[:, lanes], (((1,), (1,)), ((), ())),
                                 precision=HI, preferred_element_type=jnp.float32)
        o_h = _dot(qa_h, s0) + _dot(scores * causal, v_h)
        diag = eye * a_acc[:, lanes]
        new_ref[h] = _dot(diag, s0) + _dot(jnp.transpose(w[:, lanes]), v_h)
        meansq = jnp.mean(o_h * o_h, axis=-1, keepdims=True)
        mixed = o_h * lax.rsqrt(meansq + norm_eps) * gain * silu_g[:, lanes]
        mixed_ref[:, lanes] = mixed.astype(mixed_ref.dtype)


def mixer(acc, tok, s0, gain):
    heads, hd = s0.shape[0], s0.shape[2]
    t_len = tok.shape[0] // 4
    vmem = pl.BlockSpec(memory_space=pltpu.VMEM)
    return pl.pallas_call(
        mixer_kernel,
        out_shape=(jax.ShapeDtypeStruct(s0.shape, jnp.float32),
                   jax.ShapeDtypeStruct((t_len, heads * hd), jnp.bfloat16)),
        in_specs=[pl.BlockSpec(memory_space=pltpu.SMEM), vmem, vmem, vmem],
        out_specs=(vmem, vmem),
    )(acc, tok, s0, gain)


def route_two_stage(token_tuple, dealing):
    rows = jnp.concatenate([t[0] for t in token_tuple], axis=0)
    width = rows.shape[1]
    zn = lax.axis_size("z")
    cn = lax.axis_size("c")
    group = lax.axis_size("x") * cn
    dest = dealing[0]
    dest_col = (dest // (zn * cn)) * cn + dest % cn
    dest_row = jnp.broadcast_to((dest + 1).astype(jnp.bfloat16).reshape(1, 1), (1, width))
    payload = jnp.concatenate([rows, dest_row], axis=0)
    pick = (jnp.arange(group, dtype=jnp.int32) == dest_col)[:, None, None]
    send1 = jnp.where(pick, payload[None], jnp.zeros_like(payload)[None])
    got1 = lax.all_to_all(send1, ROW, 0, 0, tiled=False)
    held = got1[:, -1, 0].astype(jnp.int32) - 1
    body = got1[:, :-1, :]
    my_x = lax.axis_index("x")
    my_c = lax.axis_index("c")
    target = (my_x * zn + jnp.arange(zn, dtype=jnp.int32)) * cn + my_c
    match = (target[:, None] == held[None, :]).astype(jnp.bfloat16)
    send = jnp.einsum("zk,kre->zre", match, body, preferred_element_type=jnp.float32).astype(jnp.bfloat16)
    got = lax.all_to_all(send, "z", 0, 0, tiled=False)
    return jnp.sum(got.astype(jnp.float32), axis=0).astype(jnp.bfloat16)


def per_device(
    queries,
    forget_logits,
    values,
    gate_input,
    init_states,
    norm_gain,
    out_weight,
    dealing,
    accepted,
):
    local_count = queries.shape[0]
    draft_len = queries.shape[1]
    head_local = init_states.shape[1]
    head_size = init_states.shape[3]
    token_tuple = (queries, forget_logits, values, gate_input)
    mine = route_two_stage(token_tuple, dealing)
    new_states, mixed_rows = mixer(accepted, mine, init_states[0], norm_gain.reshape(1, head_size))
    new_states = new_states[None]

    mixed_rows = mixed_rows.reshape(local_count * draft_len, head_local * head_size)
    partial_out = jnp.dot(mixed_rows, out_weight, preferred_element_type=jnp.float32)
    hn = lax.axis_size("head")
    rows = partial_out.shape[0]
    split = partial_out.reshape(rows, hn, partial_out.shape[1] // hn)
    swapped = lax.all_to_all(split, "head", 1, 1, tiled=True)
    summed = jnp.sum(swapped, axis=1)
    verified = summed.astype(jnp.bfloat16).reshape(local_count, draft_len, summed.shape[1])
    return (verified, new_states)


def solution(mesh):
    xs, zs, cs = 4, mesh.shape["req"] // 8, 2
    sub = Mesh(mesh.devices.reshape(xs, zs, cs, mesh.shape["head"]), ("x", "z", "c", "head"))
    placed = (
        P(REQ, None, "head"),
        P(REQ, None, "head"),
        P(REQ, None, "head"),
        P(REQ, None, "head"),
        P(REQ, "head", None, None),
        P(),
        P("head", None),
        P(REQ),
        P(REQ),
    )
    return jax.shard_map(
        per_device,
        mesh=sub,
        in_specs=placed,
        out_specs=(P(REQ, None, "head"), P(REQ, "head", None, None)),
        check_vma=False,
    )
```

```python
import jax
import jax.numpy as jnp
from jax import lax
from jax.experimental import pallas as pl
from jax.experimental.pallas import tpu as pltpu
from jax.sharding import Mesh, PartitionSpec as P

lower_bound = 0.8
norm_eps = 1e-05

ROW = ("x", "c")
REQ = ("x", "z", "c")


HI = lax.Precision.HIGHEST


def _dot(a, b):
    return jnp.dot(a, b, precision=HI, preferred_element_type=jnp.float32)


def pack_kernel(dest_ref, q_ref, f_ref, v_ref, g_ref, out_ref):
    for i, ref in enumerate((q_ref, f_ref, v_ref, g_ref)):
        out_ref[i] = ref[0]
    mark = jnp.broadcast_to(dest_ref[0] + 1, out_ref.shape[1:]).astype(jnp.float32)
    out_ref[4] = mark.astype(out_ref.dtype)


def pack(dealing, q, f, v, g):
    vmem = pl.BlockSpec(memory_space=pltpu.VMEM)
    return pl.pallas_call(
        pack_kernel,
        out_shape=jax.ShapeDtypeStruct((5,) + q.shape[1:], q.dtype),
        in_specs=[pl.BlockSpec(memory_space=pltpu.SMEM), vmem, vmem, vmem, vmem],
        out_specs=vmem,
    )(dealing, q, f, v, g)


def mixer_kernel(acc_ref, got_ref, s0_ref, gain_ref, w_hbm, new_ref, part_ref, w_vmem, mixed_scr, sem):
    w_copy = pltpu.make_async_copy(w_hbm, w_vmem, sem)
    w_copy.start()
    acc = acc_ref[0]
    blocks = got_ref[0].astype(jnp.float32)
    for i in range(1, got_ref.shape[0]):
        blocks = blocks + got_ref[i].astype(jnp.float32)
    heads = s0_ref.shape[0]
    hd = s0_ref.shape[2]
    q = blocks[0]
    fl = blocks[1]
    v = blocks[2]
    g = blocks[3]
    t_len = q.shape[0]
    a = lower_bound + (1.0 - lower_bound) * (1.0 / (1.0 + jnp.exp(-fl)))
    b = 1.0 - a
    la = jnp.log(a)
    row = lax.broadcasted_iota(jnp.int32, (t_len, t_len), 0)
    col = lax.broadcasted_iota(jnp.int32, (t_len, t_len), 1)
    causal = (col <= row).astype(jnp.float32)
    lc = _dot(causal, la)
    big_a = jnp.exp(lc)
    inv_a = jnp.exp(-lc)
    qa = q * big_a
    ba = b * inv_a
    kept = (lax.broadcasted_iota(jnp.int32, la.shape, 0) < acc).astype(jnp.float32)
    a_acc = jnp.exp(jnp.sum(kept * la, axis=0, keepdims=True))
    w = kept * a_acc * ba
    eye_r = lax.broadcasted_iota(jnp.int32, (hd, hd), 0)
    eye_c = lax.broadcasted_iota(jnp.int32, (hd, hd), 1)
    eye = (eye_r == eye_c).astype(jnp.float32)
    gain = gain_ref[...]
    silu_g = g * (1.0 / (1.0 + jnp.exp(-g)))
    for h in range(heads):
        lanes = slice(h * hd, (h + 1) * hd)
        s0 = s0_ref[h]
        v_h = v[:, lanes]
        qa_h = qa[:, lanes]
        scores = lax.dot_general(qa_h, ba[:, lanes], (((1,), (1,)), ((), ())),
                                 precision=HI, preferred_element_type=jnp.float32)
        o_h = _dot(qa_h, s0) + _dot(scores * causal, v_h)
        diag = eye * a_acc[:, lanes]
        new_ref[h] = _dot(diag, s0) + _dot(jnp.transpose(w[:, lanes]), v_h)
        meansq = jnp.mean(o_h * o_h, axis=-1, keepdims=True)
        mixed = o_h * lax.rsqrt(meansq + norm_eps) * gain * silu_g[:, lanes]
        mixed_scr[:, lanes] = mixed.astype(mixed_scr.dtype)
    w_copy.wait()
    part_ref[...] = jnp.dot(mixed_scr[...], w_vmem[...], preferred_element_type=jnp.float32)


def mixer(acc, got, s0, gain, weight):
    heads, hd = s0.shape[0], s0.shape[2]
    t_len = got.shape[2]
    vmem = pl.BlockSpec(memory_space=pltpu.VMEM)
    return pl.pallas_call(
        mixer_kernel,
        out_shape=(jax.ShapeDtypeStruct(s0.shape, jnp.float32),
                   jax.ShapeDtypeStruct((t_len, weight.shape[1]), jnp.float32)),
        in_specs=[pl.BlockSpec(memory_space=pltpu.SMEM), vmem, vmem, vmem,
                  pl.BlockSpec(memory_space=pl.ANY)],
        out_specs=(vmem, vmem),
        scratch_shapes=[pltpu.VMEM(weight.shape, weight.dtype),
                        pltpu.VMEM((t_len, heads * hd), jnp.bfloat16),
                        pltpu.SemaphoreType.DMA(())],
    )(acc, got, s0, gain, weight)


def route_two_stage(token_tuple, dealing):
    payload = pack(dealing, *token_tuple)
    gathered = lax.all_gather(payload, ROW, axis=0, tiled=False)
    dest = gathered[:, 4, 0, 0].astype(jnp.int32) - 1
    body = gathered[:, :4]
    zn = lax.axis_size("z")
    my_x = lax.axis_index("x")
    my_c = lax.axis_index("c")
    cn = lax.axis_size("c")
    target = (my_x * zn + jnp.arange(zn, dtype=jnp.int32)) * cn + my_c
    match = (target[:, None] == dest[None, :]).astype(jnp.bfloat16)
    send = jnp.einsum("zk,kbre->zbre", match, body, preferred_element_type=jnp.float32).astype(jnp.bfloat16)
    return lax.all_to_all(send, "z", 0, 0, tiled=False)


def per_device(
    queries,
    forget_logits,
    values,
    gate_input,
    init_states,
    norm_gain,
    out_weight,
    dealing,
    accepted,
):
    local_count = queries.shape[0]
    draft_len = queries.shape[1]
    head_local = init_states.shape[1]
    head_size = init_states.shape[3]
    token_tuple = (queries, forget_logits, values, gate_input)
    got = route_two_stage(token_tuple, dealing)
    new_states, partial_out = mixer(accepted, got, init_states[0], norm_gain.reshape(1, head_size), out_weight)
    new_states = new_states[None]
    hn = lax.axis_size("head")
    rows = partial_out.shape[0]
    split = partial_out.reshape(rows, hn, partial_out.shape[1] // hn)
    swapped = lax.all_to_all(split, "head", 1, 1, tiled=True)
    summed = jnp.sum(swapped, axis=1)
    verified = summed.astype(jnp.bfloat16).reshape(local_count, draft_len, summed.shape[1])
    return (verified, new_states)


def solution(mesh):
    xs, zs, cs = 4, mesh.shape["req"] // 8, 2
    sub = Mesh(mesh.devices.reshape(xs, zs, cs, mesh.shape["head"]), ("x", "z", "c", "head"))
    placed = (
        P(REQ, None, "head"),
        P(REQ, None, "head"),
        P(REQ, None, "head"),
        P(REQ, None, "head"),
        P(REQ, "head", None, None),
        P(),
        P("head", None),
        P(REQ),
        P(REQ),
    )
    return jax.shard_map(
        per_device,
        mesh=sub,
        in_specs=placed,
        out_specs=(P(REQ, None, "head"), P(REQ, "head", None, None)),
        check_vma=False,
    )
```

```python
import jax
import jax.numpy as jnp
from jax import lax
from jax.experimental import pallas as pl
from jax.experimental.pallas import tpu as pltpu
from jax.sharding import Mesh, PartitionSpec as P

lower_bound = 0.8
norm_eps = 1e-05

ROW = ("x", "c")
REQ = ("x", "z", "c")


HI = lax.Precision.HIGHEST


def _dot(a, b):
    return jnp.dot(a, b, precision=HI, preferred_element_type=jnp.float32)


def pack_kernel(dest_ref, q_ref, f_ref, v_ref, g_ref, out_ref):
    for i, ref in enumerate((q_ref, f_ref, v_ref, g_ref)):
        out_ref[i] = ref[0]
    mark = jnp.broadcast_to(dest_ref[0] + 1, out_ref.shape[1:]).astype(jnp.float32)
    out_ref[4] = mark.astype(out_ref.dtype)


def pack(dealing, q, f, v, g):
    vmem = pl.BlockSpec(memory_space=pltpu.VMEM)
    return pl.pallas_call(
        pack_kernel,
        out_shape=jax.ShapeDtypeStruct((5,) + q.shape[1:], q.dtype),
        in_specs=[pl.BlockSpec(memory_space=pltpu.SMEM), vmem, vmem, vmem, vmem],
        out_specs=vmem,
    )(dealing, q, f, v, g)


def mixer_kernel(acc_ref, got_any, s0_ref, gain_ref, w_hbm, new_ref, part_ref, got_ref, w_vmem, mixed_scr, sems):
    got_copy = pltpu.make_async_copy(got_any, got_ref, sems.at[0])
    got_copy.start()
    w_copy = pltpu.make_async_copy(w_hbm, w_vmem, sems.at[1])
    w_copy.start()
    got_copy.wait()
    acc = acc_ref[0]
    blocks = got_ref[0].astype(jnp.float32)
    for i in range(1, got_ref.shape[0]):
        blocks = blocks + got_ref[i].astype(jnp.float32)
    heads = s0_ref.shape[0]
    hd = s0_ref.shape[2]
    q = blocks[0]
    fl = blocks[1]
    v = blocks[2]
    g = blocks[3]
    t_len = q.shape[0]
    a = lower_bound + (1.0 - lower_bound) * (1.0 / (1.0 + jnp.exp(-fl)))
    b = 1.0 - a
    la = jnp.log(a)
    row = lax.broadcasted_iota(jnp.int32, (t_len, t_len), 0)
    col = lax.broadcasted_iota(jnp.int32, (t_len, t_len), 1)
    causal = (col <= row).astype(jnp.float32)
    lc = _dot(causal, la)
    big_a = jnp.exp(lc)
    inv_a = jnp.exp(-lc)
    qa = q * big_a
    ba = b * inv_a
    kept = (lax.broadcasted_iota(jnp.int32, la.shape, 0) < acc).astype(jnp.float32)
    a_acc = jnp.exp(jnp.sum(kept * la, axis=0, keepdims=True))
    w = kept * a_acc * ba
    eye_r = lax.broadcasted_iota(jnp.int32, (hd, hd), 0)
    eye_c = lax.broadcasted_iota(jnp.int32, (hd, hd), 1)
    eye = (eye_r == eye_c).astype(jnp.float32)
    gain = gain_ref[...]
    silu_g = g * (1.0 / (1.0 + jnp.exp(-g)))
    for h in range(heads):
        lanes = slice(h * hd, (h + 1) * hd)
        s0 = s0_ref[h]
        v_h = v[:, lanes]
        qa_h = qa[:, lanes]
        scores = lax.dot_general(qa_h, ba[:, lanes], (((1,), (1,)), ((), ())),
                                 precision=HI, preferred_element_type=jnp.float32)
        o_h = _dot(qa_h, s0) + _dot(scores * causal, v_h)
        diag = eye * a_acc[:, lanes]
        new_ref[h] = _dot(diag, s0) + _dot(jnp.transpose(w[:, lanes]), v_h)
        meansq = jnp.mean(o_h * o_h, axis=-1, keepdims=True)
        mixed = o_h * lax.rsqrt(meansq + norm_eps) * gain * silu_g[:, lanes]
        mixed_scr[:, lanes] = mixed.astype(mixed_scr.dtype)
    w_copy.wait()
    chunk = part_ref.shape[2]
    mixed_all = mixed_scr[...]
    for j in range(part_ref.shape[0]):
        part_ref[j] = jnp.dot(mixed_all, w_vmem[:, j * chunk:(j + 1) * chunk],
                              preferred_element_type=jnp.float32)


def mixer(acc, got, s0, gain, weight, parts):
    heads, hd = s0.shape[0], s0.shape[2]
    t_len = got.shape[2]
    vmem = pl.BlockSpec(memory_space=pltpu.VMEM)
    anywhere = pl.BlockSpec(memory_space=pl.ANY)
    return pl.pallas_call(
        mixer_kernel,
        out_shape=(jax.ShapeDtypeStruct(s0.shape, jnp.float32),
                   jax.ShapeDtypeStruct((parts, t_len, weight.shape[1] // parts), jnp.float32)),
        in_specs=[pl.BlockSpec(memory_space=pltpu.SMEM), anywhere, vmem, vmem, anywhere],
        out_specs=(vmem, vmem),
        scratch_shapes=[pltpu.VMEM(got.shape, got.dtype),
                        pltpu.VMEM(weight.shape, weight.dtype),
                        pltpu.VMEM((t_len, heads * hd), jnp.bfloat16),
                        pltpu.SemaphoreType.DMA((2,))],
    )(acc, got, s0, gain, weight)


def select_kernel(idx_ref, held_ref, out_ref):
    count = held_ref.shape[0]
    keep = out_ref.shape[1]
    for z in range(out_ref.shape[0]):
        k = idx_ref[z]
        blk = held_ref[jnp.minimum(k, count - 1), 0:keep]
        out_ref[z] = jnp.where(k < count, blk, jnp.zeros_like(blk))


def select(idx, held, keep):
    vmem = pl.BlockSpec(memory_space=pltpu.VMEM)
    return pl.pallas_call(
        select_kernel,
        out_shape=jax.ShapeDtypeStruct((idx.shape[0], keep) + held.shape[2:], held.dtype),
        in_specs=[pl.BlockSpec(memory_space=pltpu.SMEM), vmem],
        out_specs=vmem,
    )(idx, held)


def route_two_stage(token_tuple, dealing):
    payload = pack(dealing, *token_tuple)
    gathered = lax.all_gather(payload, ROW, axis=0, tiled=False)
    dest = gathered[:, 4, 0, 0].astype(jnp.int32) - 1
    zn = lax.axis_size("z")
    my_x = lax.axis_index("x")
    my_c = lax.axis_index("c")
    cn = lax.axis_size("c")
    target = (my_x * zn + jnp.arange(zn, dtype=jnp.int32)) * cn + my_c
    count = dest.shape[0]
    slots = jnp.arange(count, dtype=jnp.int32)
    match = target[:, None] == dest[None, :]
    idx = jnp.min(jnp.where(match, slots[None, :], count), axis=1)
    send = select(idx, gathered, 4)
    return lax.all_to_all(send, "z", 0, 0, tiled=False)


def per_device(
    queries,
    forget_logits,
    values,
    gate_input,
    init_states,
    norm_gain,
    out_weight,
    dealing,
    accepted,
):
    local_count = queries.shape[0]
    draft_len = queries.shape[1]
    head_local = init_states.shape[1]
    head_size = init_states.shape[3]
    token_tuple = (queries, forget_logits, values, gate_input)
    got = route_two_stage(token_tuple, dealing)
    hn = lax.axis_size("head")
    new_states, partial_out = mixer(accepted, got, init_states[0], norm_gain.reshape(1, head_size), out_weight, hn)
    new_states = new_states[None]
    swapped = lax.all_to_all(partial_out, "head", 0, 0, tiled=True)
    summed = jnp.sum(swapped, axis=0)
    verified = summed.astype(jnp.bfloat16).reshape(local_count, draft_len, summed.shape[1])
    return (verified, new_states)


def solution(mesh):
    xs, zs, cs = 4, mesh.shape["req"] // 8, 2
    sub = Mesh(mesh.devices.reshape(xs, zs, cs, mesh.shape["head"]), ("x", "z", "c", "head"))
    placed = (
        P(REQ, None, "head"),
        P(REQ, None, "head"),
        P(REQ, None, "head"),
        P(REQ, None, "head"),
        P(REQ, "head", None, None),
        P(),
        P("head", None),
        P(REQ),
        P(REQ),
    )
    return jax.shard_map(
        per_device,
        mesh=sub,
        in_specs=placed,
        out_specs=(P(REQ, None, "head"), P(REQ, "head", None, None)),
        check_vma=False,
    )
```

```python
import jax
import jax.numpy as jnp
from jax import lax
from jax.experimental import pallas as pl
from jax.experimental.pallas import tpu as pltpu
from jax.sharding import Mesh, PartitionSpec as P

lower_bound = 0.8
norm_eps = 1e-05

ROW = ("x", "c")
REQ = ("x", "z", "c")


HI = lax.Precision.HIGHEST


def _dot(a, b):
    return jnp.dot(a, b, precision=HI, preferred_element_type=jnp.float32)


def pack_kernel(dest_ref, q_ref, f_ref, v_ref, g_ref, out_ref):
    for i, ref in enumerate((q_ref, f_ref, v_ref, g_ref)):
        out_ref[i] = ref[0]
    mark = jnp.broadcast_to(dest_ref[0] + 1, out_ref.shape[1:]).astype(jnp.float32)
    out_ref[4] = mark.astype(out_ref.dtype)


def pack(dealing, q, f, v, g):
    vmem = pl.BlockSpec(memory_space=pltpu.VMEM)
    return pl.pallas_call(
        pack_kernel,
        out_shape=jax.ShapeDtypeStruct((5,) + q.shape[1:], q.dtype),
        in_specs=[pl.BlockSpec(memory_space=pltpu.SMEM), vmem, vmem, vmem, vmem],
        out_specs=vmem,
    )(dealing, q, f, v, g)


def mixer_kernel(acc_ref, tok_ref, s0_ref, gain_ref, w_hbm, new_ref, part_ref, w_vmem, mixed_scr, sem):
    w_copy = pltpu.make_async_copy(w_hbm, w_vmem, sem)
    w_copy.start()
    acc = acc_ref[0]
    blocks = tok_ref[...].astype(jnp.float32)
    heads = s0_ref.shape[0]
    hd = s0_ref.shape[2]
    q = blocks[0]
    fl = blocks[1]
    v = blocks[2]
    g = blocks[3]
    t_len = q.shape[0]
    a = lower_bound + (1.0 - lower_bound) * (1.0 / (1.0 + jnp.exp(-fl)))
    b = 1.0 - a
    la = jnp.log(a)
    row = lax.broadcasted_iota(jnp.int32, (t_len, t_len), 0)
    col = lax.broadcasted_iota(jnp.int32, (t_len, t_len), 1)
    causal = (col <= row).astype(jnp.float32)
    lc = _dot(causal, la)
    big_a = jnp.exp(lc)
    inv_a = jnp.exp(-lc)
    qa = q * big_a
    ba = b * inv_a
    kept = (lax.broadcasted_iota(jnp.int32, la.shape, 0) < acc).astype(jnp.float32)
    a_acc = jnp.exp(jnp.sum(kept * la, axis=0, keepdims=True))
    w = kept * a_acc * ba
    eye_r = lax.broadcasted_iota(jnp.int32, (hd, hd), 0)
    eye_c = lax.broadcasted_iota(jnp.int32, (hd, hd), 1)
    eye = (eye_r == eye_c).astype(jnp.float32)
    gain = gain_ref[...]
    silu_g = g * (1.0 / (1.0 + jnp.exp(-g)))
    for h in range(heads):
        lanes = slice(h * hd, (h + 1) * hd)
        s0 = s0_ref[h]
        v_h = v[:, lanes]
        qa_h = qa[:, lanes]
        scores = lax.dot_general(qa_h, ba[:, lanes], (((1,), (1,)), ((), ())),
                                 precision=HI, preferred_element_type=jnp.float32)
        o_h = _dot(qa_h, s0) + _dot(scores * causal, v_h)
        diag = eye * a_acc[:, lanes]
        new_ref[h] = _dot(diag, s0) + _dot(jnp.transpose(w[:, lanes]), v_h)
        meansq = jnp.mean(o_h * o_h, axis=-1, keepdims=True)
        mixed = o_h * lax.rsqrt(meansq + norm_eps) * gain * silu_g[:, lanes]
        mixed_scr[:, lanes] = mixed.astype(mixed_scr.dtype)
    w_copy.wait()
    chunk = part_ref.shape[2]
    mixed_all = mixed_scr[...]
    for j in range(part_ref.shape[0]):
        part_ref[j] = jnp.dot(mixed_all, w_vmem[:, j * chunk:(j + 1) * chunk],
                              preferred_element_type=jnp.float32)


def mixer(acc, tok, s0, gain, weight, parts):
    heads, hd = s0.shape[0], s0.shape[2]
    t_len = tok.shape[1]
    vmem = pl.BlockSpec(memory_space=pltpu.VMEM)
    return pl.pallas_call(
        mixer_kernel,
        out_shape=(jax.ShapeDtypeStruct(s0.shape, jnp.float32),
                   jax.ShapeDtypeStruct((parts, t_len, weight.shape[1] // parts), jnp.float32)),
        in_specs=[pl.BlockSpec(memory_space=pltpu.SMEM), vmem, vmem, vmem,
                  pl.BlockSpec(memory_space=pl.ANY)],
        out_specs=(vmem, vmem),
        scratch_shapes=[pltpu.VMEM(weight.shape, weight.dtype),
                        pltpu.VMEM((t_len, heads * hd), jnp.bfloat16),
                        pltpu.SemaphoreType.DMA(())],
    )(acc, tok, s0, gain, weight)


def route_two_stage(token_tuple, dealing):
    payload = pack(dealing, *token_tuple)
    gathered = lax.all_gather(payload, ROW, axis=0, tiled=False)
    dest = gathered[:, 4, 0, 0].astype(jnp.int32) - 1
    body = gathered[:, :4]
    zn = lax.axis_size("z")
    my_x = lax.axis_index("x")
    my_c = lax.axis_index("c")
    cn = lax.axis_size("c")
    target = (my_x * zn + jnp.arange(zn, dtype=jnp.int32)) * cn + my_c
    count = dest.shape[0]
    slots = jnp.arange(count, dtype=jnp.int32)
    idx = jnp.min(jnp.where(target[:, None] == dest[None, :], slots[None, :], count), axis=1)
    send = jnp.take(body, idx, axis=0, mode="fill", fill_value=0)
    got = lax.all_to_all(send, "z", 0, 0, tiled=False)
    return jnp.sum(got.astype(jnp.float32), axis=0).astype(jnp.bfloat16)


def per_device(
    queries,
    forget_logits,
    values,
    gate_input,
    init_states,
    norm_gain,
    out_weight,
    dealing,
    accepted,
):
    local_count = queries.shape[0]
    draft_len = queries.shape[1]
    head_local = init_states.shape[1]
    head_size = init_states.shape[3]
    token_tuple = (queries, forget_logits, values, gate_input)
    got = route_two_stage(token_tuple, dealing)
    hn = lax.axis_size("head")
    new_states, partial_out = mixer(accepted, got, init_states[0], norm_gain.reshape(1, head_size), out_weight, hn)
    new_states = new_states[None]
    swapped = lax.all_to_all(partial_out, "head", 0, 0, tiled=True)
    summed = jnp.sum(swapped, axis=0)
    verified = summed.astype(jnp.bfloat16).reshape(local_count, draft_len, summed.shape[1])
    return (verified, new_states)


def solution(mesh):
    xs, zs, cs = 4, mesh.shape["req"] // 8, 2
    sub = Mesh(mesh.devices.reshape(xs, zs, cs, mesh.shape["head"]), ("x", "z", "c", "head"))
    placed = (
        P(REQ, None, "head"),
        P(REQ, None, "head"),
        P(REQ, None, "head"),
        P(REQ, None, "head"),
        P(REQ, "head", None, None),
        P(),
        P("head", None),
        P(REQ),
        P(REQ),
    )
    return jax.shard_map(
        per_device,
        mesh=sub,
        in_specs=placed,
        out_specs=(P(REQ, None, "head"), P(REQ, "head", None, None)),
        check_vma=False,
    )
```

```python
import jax
import jax.numpy as jnp
from jax import lax
from jax.experimental import pallas as pl
from jax.experimental.pallas import tpu as pltpu
from jax.sharding import Mesh, PartitionSpec as P

lower_bound = 0.8
norm_eps = 1e-05

ROW = ("x", "c")
REQ = ("x", "z", "c")


HI = lax.Precision.HIGHEST


def _dot(a, b):
    return jnp.dot(a, b, precision=HI, preferred_element_type=jnp.float32)


def pack_kernel(dest_ref, q_ref, f_ref, v_ref, g_ref, out_ref):
    for i, ref in enumerate((q_ref, f_ref, v_ref, g_ref)):
        out_ref[i] = ref[0]
    mark = jnp.broadcast_to(dest_ref[0] + 1, out_ref.shape[1:]).astype(jnp.float32)
    out_ref[4] = mark.astype(out_ref.dtype)


def pack(dealing, q, f, v, g):
    vmem = pl.BlockSpec(memory_space=pltpu.VMEM)
    return pl.pallas_call(
        pack_kernel,
        out_shape=jax.ShapeDtypeStruct((5,) + q.shape[1:], q.dtype),
        in_specs=[pl.BlockSpec(memory_space=pltpu.SMEM), vmem, vmem, vmem, vmem],
        out_specs=vmem,
    )(dealing, q, f, v, g)


def mixer_kernel(acc_ref, tok_ref, s0_ref, gain_ref, w_hbm, new_ref, part_ref, w_vmem, mixed_scr, sem):
    w_copy = pltpu.make_async_copy(w_hbm, w_vmem, sem)
    w_copy.start()
    acc = acc_ref[0]
    blocks = tok_ref[...].astype(jnp.float32)
    heads = s0_ref.shape[0]
    hd = s0_ref.shape[2]
    q = blocks[0]
    fl = blocks[1]
    v = blocks[2]
    g = blocks[3]
    t_len = q.shape[0]
    a = lower_bound + (1.0 - lower_bound) * (1.0 / (1.0 + jnp.exp(-fl)))
    b = 1.0 - a
    la = jnp.log(a)
    row = lax.broadcasted_iota(jnp.int32, (t_len, t_len), 0)
    col = lax.broadcasted_iota(jnp.int32, (t_len, t_len), 1)
    causal = (col <= row).astype(jnp.float32)
    lc = _dot(causal, la)
    big_a = jnp.exp(lc)
    inv_a = jnp.exp(-lc)
    qa = q * big_a
    ba = b * inv_a
    kept_t = (lax.broadcasted_iota(jnp.int32, (la.shape[1], t_len), 1) < acc).astype(jnp.float32)
    a_col = jnp.exp(jnp.sum(kept_t * jnp.transpose(la), axis=1, keepdims=True))
    w_t = kept_t * a_col * jnp.transpose(ba)
    gain = gain_ref[...]
    silu_g = g * (1.0 / (1.0 + jnp.exp(-g)))
    for h in range(heads):
        lanes = slice(h * hd, (h + 1) * hd)
        s0 = s0_ref[h]
        v_h = v[:, lanes]
        qa_h = qa[:, lanes]
        scores = lax.dot_general(qa_h, ba[:, lanes], (((1,), (1,)), ((), ())),
                                 precision=HI, preferred_element_type=jnp.float32)
        o_h = _dot(qa_h, s0) + _dot(scores * causal, v_h)
        new_ref[h] = a_col[lanes] * s0 + _dot(w_t[lanes], v_h)
        meansq = jnp.mean(o_h * o_h, axis=-1, keepdims=True)
        mixed = o_h * lax.rsqrt(meansq + norm_eps) * gain * silu_g[:, lanes]
        mixed_scr[:, lanes] = mixed.astype(mixed_scr.dtype)
    w_copy.wait()
    chunk = part_ref.shape[2]
    mixed_all = mixed_scr[...]
    for j in range(part_ref.shape[0]):
        part_ref[j] = jnp.dot(mixed_all, w_vmem[:, j * chunk:(j + 1) * chunk],
                              preferred_element_type=jnp.float32)


def mixer(acc, tok, s0, gain, weight, parts):
    heads, hd = s0.shape[0], s0.shape[2]
    t_len = tok.shape[1]
    vmem = pl.BlockSpec(memory_space=pltpu.VMEM)
    return pl.pallas_call(
        mixer_kernel,
        out_shape=(jax.ShapeDtypeStruct(s0.shape, jnp.float32),
                   jax.ShapeDtypeStruct((parts, t_len, weight.shape[1] // parts), jnp.float32)),
        in_specs=[pl.BlockSpec(memory_space=pltpu.SMEM), vmem, vmem, vmem,
                  pl.BlockSpec(memory_space=pl.ANY)],
        out_specs=(vmem, vmem),
        scratch_shapes=[pltpu.VMEM(weight.shape, weight.dtype),
                        pltpu.VMEM((t_len, heads * hd), jnp.bfloat16),
                        pltpu.SemaphoreType.DMA(())],
    )(acc, tok, s0, gain, weight)


def route_two_stage(token_tuple, dealing):
    payload = pack(dealing, *token_tuple)
    gathered = lax.all_gather(payload, ROW, axis=0, tiled=False)
    dest = gathered[:, 4, 0, 0].astype(jnp.int32) - 1
    body = gathered[:, :4]
    zn = lax.axis_size("z")
    my_x = lax.axis_index("x")
    my_c = lax.axis_index("c")
    cn = lax.axis_size("c")
    target = (my_x * zn + jnp.arange(zn, dtype=jnp.int32)) * cn + my_c
    count = dest.shape[0]
    slots = jnp.arange(count, dtype=jnp.int32)
    idx = jnp.min(jnp.where(target[:, None] == dest[None, :], slots[None, :], count), axis=1)
    send = jnp.take(body, idx, axis=0, mode="fill", fill_value=0)
    got = lax.all_to_all(send, "z", 0, 0, tiled=False)
    return jnp.sum(got.astype(jnp.float32), axis=0).astype(jnp.bfloat16)


def per_device(
    queries,
    forget_logits,
    values,
    gate_input,
    init_states,
    norm_gain,
    out_weight,
    dealing,
    accepted,
):
    local_count = queries.shape[0]
    draft_len = queries.shape[1]
    head_local = init_states.shape[1]
    head_size = init_states.shape[3]
    token_tuple = (queries, forget_logits, values, gate_input)
    got = route_two_stage(token_tuple, dealing)
    hn = lax.axis_size("head")
    new_states, partial_out = mixer(accepted, got, init_states[0], norm_gain.reshape(1, head_size), out_weight, hn)
    new_states = new_states[None]
    swapped = lax.all_to_all(partial_out, "head", 0, 0, tiled=True)
    summed = jnp.sum(swapped, axis=0)
    verified = summed.astype(jnp.bfloat16).reshape(local_count, draft_len, summed.shape[1])
    return (verified, new_states)


def solution(mesh):
    xs, zs, cs = 4, mesh.shape["req"] // 8, 2
    sub = Mesh(mesh.devices.reshape(xs, zs, cs, mesh.shape["head"]), ("x", "z", "c", "head"))
    placed = (
        P(REQ, None, "head"),
        P(REQ, None, "head"),
        P(REQ, None, "head"),
        P(REQ, None, "head"),
        P(REQ, "head", None, None),
        P(),
        P("head", None),
        P(REQ),
        P(REQ),
    )
    return jax.shard_map(
        per_device,
        mesh=sub,
        in_specs=placed,
        out_specs=(P(REQ, None, "head"), P(REQ, "head", None, None)),
        check_vma=False,
    )
```

```python
import jax
import jax.numpy as jnp
from jax import lax
from jax.experimental import pallas as pl
from jax.experimental.pallas import tpu as pltpu
from jax.sharding import Mesh, PartitionSpec as P

lower_bound = 0.8
norm_eps = 1e-05

ROW = ("x", "c")
REQ = ("x", "zh", "zl", "c")


HI = lax.Precision.HIGHEST


def _dot(a, b):
    return jnp.dot(a, b, precision=HI, preferred_element_type=jnp.float32)


def pack_kernel(dest_ref, q_ref, f_ref, v_ref, g_ref, out_ref):
    for i, ref in enumerate((q_ref, f_ref, v_ref, g_ref)):
        out_ref[i] = ref[0]
    mark = jnp.broadcast_to(dest_ref[0] + 1, out_ref.shape[1:]).astype(jnp.float32)
    out_ref[4] = mark.astype(out_ref.dtype)


def pack(dealing, q, f, v, g):
    vmem = pl.BlockSpec(memory_space=pltpu.VMEM)
    return pl.pallas_call(
        pack_kernel,
        out_shape=jax.ShapeDtypeStruct((5,) + q.shape[1:], q.dtype),
        in_specs=[pl.BlockSpec(memory_space=pltpu.SMEM), vmem, vmem, vmem, vmem],
        out_specs=vmem,
    )(dealing, q, f, v, g)


def mixer_kernel(acc_ref, tok_ref, s0_ref, gain_ref, w_hbm, new_ref, part_ref, w_vmem, mixed_scr, sem):
    w_copy = pltpu.make_async_copy(w_hbm, w_vmem, sem)
    w_copy.start()
    acc = acc_ref[0]
    blocks = tok_ref[...].astype(jnp.float32)
    heads = s0_ref.shape[0]
    hd = s0_ref.shape[2]
    q = blocks[0]
    fl = blocks[1]
    v = blocks[2]
    g = blocks[3]
    t_len = q.shape[0]
    a = lower_bound + (1.0 - lower_bound) * (1.0 / (1.0 + jnp.exp(-fl)))
    b = 1.0 - a
    la = jnp.log(a)
    row = lax.broadcasted_iota(jnp.int32, (t_len, t_len), 0)
    col = lax.broadcasted_iota(jnp.int32, (t_len, t_len), 1)
    causal = (col <= row).astype(jnp.float32)
    lc = _dot(causal, la)
    big_a = jnp.exp(lc)
    inv_a = jnp.exp(-lc)
    qa = q * big_a
    ba = b * inv_a
    kept_t = (lax.broadcasted_iota(jnp.int32, (la.shape[1], t_len), 1) < acc).astype(jnp.float32)
    a_col = jnp.exp(jnp.sum(kept_t * jnp.transpose(la), axis=1, keepdims=True))
    w_t = kept_t * a_col * jnp.transpose(ba)
    gain = gain_ref[...]
    silu_g = g * (1.0 / (1.0 + jnp.exp(-g)))
    for h in range(heads):
        lanes = slice(h * hd, (h + 1) * hd)
        s0 = s0_ref[h]
        v_h = v[:, lanes]
        qa_h = qa[:, lanes]
        scores = lax.dot_general(qa_h, ba[:, lanes], (((1,), (1,)), ((), ())),
                                 precision=HI, preferred_element_type=jnp.float32)
        o_h = _dot(qa_h, s0) + _dot(scores * causal, v_h)
        new_ref[h] = a_col[lanes] * s0 + _dot(w_t[lanes], v_h)
        meansq = jnp.mean(o_h * o_h, axis=-1, keepdims=True)
        mixed = o_h * lax.rsqrt(meansq + norm_eps) * gain * silu_g[:, lanes]
        mixed_scr[:, lanes] = mixed.astype(mixed_scr.dtype)
    w_copy.wait()
    chunk = part_ref.shape[2]
    mixed_all = mixed_scr[...]
    for j in range(part_ref.shape[0]):
        part_ref[j] = jnp.dot(mixed_all, w_vmem[:, j * chunk:(j + 1) * chunk],
                              preferred_element_type=jnp.float32)


def mixer(acc, tok, s0, gain, weight, parts):
    heads, hd = s0.shape[0], s0.shape[2]
    t_len = tok.shape[1]
    vmem = pl.BlockSpec(memory_space=pltpu.VMEM)
    return pl.pallas_call(
        mixer_kernel,
        out_shape=(jax.ShapeDtypeStruct(s0.shape, jnp.float32),
                   jax.ShapeDtypeStruct((parts, t_len, weight.shape[1] // parts), jnp.float32)),
        in_specs=[pl.BlockSpec(memory_space=pltpu.SMEM), vmem, vmem, vmem,
                  pl.BlockSpec(memory_space=pl.ANY)],
        out_specs=(vmem, vmem),
        scratch_shapes=[pltpu.VMEM(weight.shape, weight.dtype),
                        pltpu.VMEM((t_len, heads * hd), jnp.bfloat16),
                        pltpu.SemaphoreType.DMA(())],
    )(acc, tok, s0, gain, weight)


def route_two_stage(token_tuple, dealing):
    payload = pack(dealing, *token_tuple)
    gathered = lax.all_gather(payload, ROW, axis=0, tiled=False)
    dest = gathered[:, 4, 0, 0].astype(jnp.int32) - 1
    body = gathered[:, :4]
    zh_n = lax.axis_size("zh")
    zl_n = lax.axis_size("zl")
    zn = zh_n * zl_n
    my_x = lax.axis_index("x")
    my_c = lax.axis_index("c")
    cn = lax.axis_size("c")
    target = (my_x * zn + jnp.arange(zn, dtype=jnp.int32)) * cn + my_c
    count = dest.shape[0]
    slots = jnp.arange(count, dtype=jnp.int32)
    idx = jnp.min(jnp.where(target[:, None] == dest[None, :], slots[None, :], count), axis=1)
    send = jnp.take(body, idx, axis=0, mode="fill", fill_value=0)
    send = send.reshape((zh_n, zl_n) + send.shape[1:])
    got = lax.all_to_all(send, "zl", 1, 1, tiled=False)
    part = jnp.sum(got.astype(jnp.float32), axis=1).astype(jnp.bfloat16)
    got = lax.all_to_all(part, "zh", 0, 0, tiled=False)
    return jnp.sum(got.astype(jnp.float32), axis=0).astype(jnp.bfloat16)


def per_device(
    queries,
    forget_logits,
    values,
    gate_input,
    init_states,
    norm_gain,
    out_weight,
    dealing,
    accepted,
):
    local_count = queries.shape[0]
    draft_len = queries.shape[1]
    head_local = init_states.shape[1]
    head_size = init_states.shape[3]
    token_tuple = (queries, forget_logits, values, gate_input)
    got = route_two_stage(token_tuple, dealing)
    hn = lax.axis_size("head")
    new_states, partial_out = mixer(accepted, got, init_states[0], norm_gain.reshape(1, head_size), out_weight, hn)
    new_states = new_states[None]
    swapped = lax.all_to_all(partial_out, "head", 0, 0, tiled=True)
    summed = jnp.sum(swapped, axis=0)
    verified = summed.astype(jnp.bfloat16).reshape(local_count, draft_len, summed.shape[1])
    return (verified, new_states)


def solution(mesh):
    xs, cs, zl = 4, 2, 4
    zh = mesh.shape["req"] // (xs * cs * zl)
    sub = Mesh(mesh.devices.reshape(xs, zh, zl, cs, mesh.shape["head"]), ("x", "zh", "zl", "c", "head"))
    placed = (
        P(REQ, None, "head"),
        P(REQ, None, "head"),
        P(REQ, None, "head"),
        P(REQ, None, "head"),
        P(REQ, "head", None, None),
        P(),
        P("head", None),
        P(REQ),
        P(REQ),
    )
    return jax.shard_map(
        per_device,
        mesh=sub,
        in_specs=placed,
        out_specs=(P(REQ, None, "head"), P(REQ, "head", None, None)),
        check_vma=False,
    )
```

```python
import jax
import jax.numpy as jnp
from jax import lax
from jax.experimental import pallas as pl
from jax.experimental.pallas import tpu as pltpu
from jax.sharding import Mesh, PartitionSpec as P

lower_bound = 0.8
norm_eps = 1e-05

ROW = ("x", "c")
REQ = ("x", "zh", "zl", "c")


HI = lax.Precision.HIGHEST


def _dot(a, b):
    return jnp.dot(a, b, precision=HI, preferred_element_type=jnp.float32)


def mixer_kernel(acc_ref, tok_ref, s0_ref, gain_ref, w_hbm, new_ref, part_ref, w_vmem, mixed_scr, sem):
    w_copy = pltpu.make_async_copy(w_hbm, w_vmem, sem)
    w_copy.start()
    acc = acc_ref[0]
    blocks = tok_ref[...].astype(jnp.float32)
    heads = s0_ref.shape[0]
    hd = s0_ref.shape[2]
    q = blocks[0]
    fl = blocks[1]
    v = blocks[2]
    g = blocks[3]
    t_len = q.shape[0]
    a = lower_bound + (1.0 - lower_bound) * (1.0 / (1.0 + jnp.exp(-fl)))
    b = 1.0 - a
    la = jnp.log(a)
    row = lax.broadcasted_iota(jnp.int32, (t_len, t_len), 0)
    col = lax.broadcasted_iota(jnp.int32, (t_len, t_len), 1)
    causal = (col <= row).astype(jnp.float32)
    lc = _dot(causal, la)
    big_a = jnp.exp(lc)
    inv_a = jnp.exp(-lc)
    qa = q * big_a
    ba = b * inv_a
    kept_t = (lax.broadcasted_iota(jnp.int32, (la.shape[1], t_len), 1) < acc).astype(jnp.float32)
    a_col = jnp.exp(jnp.sum(kept_t * jnp.transpose(la), axis=1, keepdims=True))
    w_t = kept_t * a_col * jnp.transpose(ba)
    gain = gain_ref[...]
    silu_g = g * (1.0 / (1.0 + jnp.exp(-g)))
    for h in range(heads):
        lanes = slice(h * hd, (h + 1) * hd)
        s0 = s0_ref[h]
        v_h = v[:, lanes]
        qa_h = qa[:, lanes]
        scores = lax.dot_general(qa_h, ba[:, lanes], (((1,), (1,)), ((), ())),
                                 precision=HI, preferred_element_type=jnp.float32)
        o_h = _dot(qa_h, s0) + _dot(scores * causal, v_h)
        new_ref[h] = a_col[lanes] * s0 + _dot(w_t[lanes], v_h)
        meansq = jnp.mean(o_h * o_h, axis=-1, keepdims=True)
        mixed = o_h * lax.rsqrt(meansq + norm_eps) * gain * silu_g[:, lanes]
        mixed_scr[:, lanes] = mixed.astype(mixed_scr.dtype)
    w_copy.wait()
    chunk = part_ref.shape[2]
    mixed_all = mixed_scr[...]
    for j in range(part_ref.shape[0]):
        part_ref[j] = jnp.dot(mixed_all, w_vmem[:, j * chunk:(j + 1) * chunk],
                              preferred_element_type=jnp.float32)


def mixer(acc, tok, s0, gain, weight, parts):
    heads, hd = s0.shape[0], s0.shape[2]
    t_len = tok.shape[1]
    vmem = pl.BlockSpec(memory_space=pltpu.VMEM)
    return pl.pallas_call(
        mixer_kernel,
        out_shape=(jax.ShapeDtypeStruct(s0.shape, jnp.float32),
                   jax.ShapeDtypeStruct((parts, t_len, weight.shape[1] // parts), jnp.float32)),
        in_specs=[pl.BlockSpec(memory_space=pltpu.SMEM), vmem, vmem, vmem,
                  pl.BlockSpec(memory_space=pl.ANY)],
        out_specs=(vmem, vmem),
        scratch_shapes=[pltpu.VMEM(weight.shape, weight.dtype),
                        pltpu.VMEM((t_len, heads * hd), jnp.bfloat16),
                        pltpu.SemaphoreType.DMA(())],
    )(acc, tok, s0, gain, weight)


def route_two_stage(token_tuple, dealing):
    shape = (len(token_tuple) + 1,) + token_tuple[0].shape[1:]
    block = lax.broadcasted_iota(jnp.int32, shape, 0)
    payload = jnp.broadcast_to((dealing[0] + 1).astype(jnp.bfloat16), shape)
    for i, t in enumerate(token_tuple):
        payload = jnp.where(block == i, t, payload)
    gathered = lax.all_gather(payload, ROW, axis=0, tiled=False)
    dest = gathered[:, 4, 0, 0].astype(jnp.int32) - 1
    body = gathered[:, :4]
    zh_n = lax.axis_size("zh")
    zl_n = lax.axis_size("zl")
    zn = zh_n * zl_n
    my_x = lax.axis_index("x")
    my_c = lax.axis_index("c")
    cn = lax.axis_size("c")
    target = (my_x * zn + jnp.arange(zn, dtype=jnp.int32)) * cn + my_c
    count = dest.shape[0]
    slots = jnp.arange(count, dtype=jnp.int32)
    idx = jnp.min(jnp.where(target[:, None] == dest[None, :], slots[None, :], count), axis=1)
    send = jnp.take(body, idx, axis=0, mode="fill", fill_value=0)
    send = send.reshape((zh_n, zl_n) + send.shape[1:])
    got = lax.all_to_all(send, "zl", 1, 1, tiled=False)
    part = jnp.sum(got.astype(jnp.float32), axis=1).astype(jnp.bfloat16)
    got = lax.all_to_all(part, "zh", 0, 0, tiled=False)
    return jnp.sum(got.astype(jnp.float32), axis=0).astype(jnp.bfloat16)


def per_device(
    queries,
    forget_logits,
    values,
    gate_input,
    init_states,
    norm_gain,
    out_weight,
    dealing,
    accepted,
):
    local_count = queries.shape[0]
    draft_len = queries.shape[1]
    head_local = init_states.shape[1]
    head_size = init_states.shape[3]
    token_tuple = (queries, forget_logits, values, gate_input)
    got = route_two_stage(token_tuple, dealing)
    hn = lax.axis_size("head")
    new_states, partial_out = mixer(accepted, got, init_states[0], norm_gain.reshape(1, head_size), out_weight, hn)
    new_states = new_states[None]
    swapped = lax.all_to_all(partial_out, "head", 0, 0, tiled=True)
    summed = jnp.sum(swapped, axis=0)
    verified = summed.astype(jnp.bfloat16).reshape(local_count, draft_len, summed.shape[1])
    return (verified, new_states)


def solution(mesh):
    xs, cs, zl = 4, 2, 4
    zh = mesh.shape["req"] // (xs * cs * zl)
    sub = Mesh(mesh.devices.reshape(xs, zh, zl, cs, mesh.shape["head"]), ("x", "zh", "zl", "c", "head"))
    placed = (
        P(REQ, None, "head"),
        P(REQ, None, "head"),
        P(REQ, None, "head"),
        P(REQ, None, "head"),
        P(REQ, "head", None, None),
        P(),
        P("head", None),
        P(REQ),
        P(REQ),
    )
    return jax.shard_map(
        per_device,
        mesh=sub,
        in_specs=placed,
        out_specs=(P(REQ, None, "head"), P(REQ, "head", None, None)),
        check_vma=False,
    )
```

```python
import jax
import jax.numpy as jnp
from jax import lax
from jax.experimental import pallas as pl
from jax.experimental.pallas import tpu as pltpu
from jax.sharding import Mesh, PartitionSpec as P

lower_bound = 0.8
norm_eps = 1e-05

ROW = ("x", "c")
REQ = ("x", "zh", "zl", "c")


HI = lax.Precision.HIGHEST


def _dot(a, b):
    return jnp.dot(a, b, precision=HI, preferred_element_type=jnp.float32)


def mixer_kernel(tok_ref, s0_ref, gain_ref, w_hbm, part_ref, w_vmem, mixed_scr, sem):
    w_copy = pltpu.make_async_copy(w_hbm, w_vmem, sem)
    w_copy.start()
    blocks = tok_ref[...].astype(jnp.float32)
    heads = s0_ref.shape[0]
    hd = s0_ref.shape[2]
    q = blocks[0]
    fl = blocks[1]
    v = blocks[2]
    g = blocks[3]
    t_len = q.shape[0]
    a = lower_bound + (1.0 - lower_bound) * (1.0 / (1.0 + jnp.exp(-fl)))
    b = 1.0 - a
    la = jnp.log(a)
    row = lax.broadcasted_iota(jnp.int32, (t_len, t_len), 0)
    col = lax.broadcasted_iota(jnp.int32, (t_len, t_len), 1)
    causal = (col <= row).astype(jnp.float32)
    lc = _dot(causal, la)
    big_a = jnp.exp(lc)
    inv_a = jnp.exp(-lc)
    qa = q * big_a
    ba = b * inv_a
    gain = gain_ref[...]
    silu_g = g * (1.0 / (1.0 + jnp.exp(-g)))
    for h in range(heads):
        lanes = slice(h * hd, (h + 1) * hd)
        s0 = s0_ref[h]
        v_h = v[:, lanes]
        qa_h = qa[:, lanes]
        scores = lax.dot_general(qa_h, ba[:, lanes], (((1,), (1,)), ((), ())),
                                 precision=HI, preferred_element_type=jnp.float32)
        o_h = _dot(qa_h, s0) + _dot(scores * causal, v_h)
        meansq = jnp.mean(o_h * o_h, axis=-1, keepdims=True)
        mixed = o_h * lax.rsqrt(meansq + norm_eps) * gain * silu_g[:, lanes]
        mixed_scr[:, lanes] = mixed.astype(mixed_scr.dtype)
    w_copy.wait()
    chunk = part_ref.shape[2]
    mixed_all = mixed_scr[...]
    for j in range(part_ref.shape[0]):
        part_ref[j] = jnp.dot(mixed_all, w_vmem[:, j * chunk:(j + 1) * chunk],
                              preferred_element_type=jnp.float32)


def state_kernel(acc_ref, tok_ref, s0_ref, new_ref):
    acc = acc_ref[0]
    fl = tok_ref[1].astype(jnp.float32)
    v = tok_ref[2].astype(jnp.float32)
    t_len = fl.shape[0]
    hd = s0_ref.shape[2]
    a = lower_bound + (1.0 - lower_bound) * (1.0 / (1.0 + jnp.exp(-fl)))
    b = 1.0 - a
    la = jnp.log(a)
    row = lax.broadcasted_iota(jnp.int32, (t_len, t_len), 0)
    col = lax.broadcasted_iota(jnp.int32, (t_len, t_len), 1)
    causal = (col <= row).astype(jnp.float32)
    inv_a = jnp.exp(-_dot(causal, la))
    ba = b * inv_a
    kept_t = (lax.broadcasted_iota(jnp.int32, (la.shape[1], t_len), 1) < acc).astype(jnp.float32)
    a_col = jnp.exp(jnp.sum(kept_t * jnp.transpose(la), axis=1, keepdims=True))
    w_t = kept_t * a_col * jnp.transpose(ba)
    for h in range(s0_ref.shape[0]):
        lanes = slice(h * hd, (h + 1) * hd)
        new_ref[h] = a_col[lanes] * s0_ref[h] + _dot(w_t[lanes], v[:, lanes])


def new_state(acc, tok, s0):
    vmem = pl.BlockSpec(memory_space=pltpu.VMEM)
    return pl.pallas_call(
        state_kernel,
        out_shape=jax.ShapeDtypeStruct(s0.shape, jnp.float32),
        in_specs=[pl.BlockSpec(memory_space=pltpu.SMEM), vmem, vmem],
        out_specs=vmem,
    )(acc, tok, s0)


def mixer(tok, s0, gain, weight, parts):
    heads, hd = s0.shape[0], s0.shape[2]
    t_len = tok.shape[1]
    vmem = pl.BlockSpec(memory_space=pltpu.VMEM)
    return pl.pallas_call(
        mixer_kernel,
        out_shape=jax.ShapeDtypeStruct((parts, t_len, weight.shape[1] // parts), jnp.float32),
        in_specs=[vmem, vmem, vmem, pl.BlockSpec(memory_space=pl.ANY)],
        out_specs=vmem,
        scratch_shapes=[pltpu.VMEM(weight.shape, weight.dtype),
                        pltpu.VMEM((t_len, heads * hd), jnp.bfloat16),
                        pltpu.SemaphoreType.DMA(())],
    )(tok, s0, gain, weight)


def route_two_stage(token_tuple, dealing):
    shape = (len(token_tuple) + 1,) + token_tuple[0].shape[1:]
    block = lax.broadcasted_iota(jnp.int32, shape, 0)
    payload = jnp.broadcast_to((dealing[0] + 1).astype(jnp.bfloat16), shape)
    for i, t in enumerate(token_tuple):
        payload = jnp.where(block == i, t, payload)
    gathered = lax.all_gather(payload, ROW, axis=0, tiled=False)
    dest = gathered[:, 4, 0, 0].astype(jnp.int32) - 1
    body = gathered[:, :4]
    zh_n = lax.axis_size("zh")
    zl_n = lax.axis_size("zl")
    zn = zh_n * zl_n
    my_x = lax.axis_index("x")
    my_c = lax.axis_index("c")
    cn = lax.axis_size("c")
    target = (my_x * zn + jnp.arange(zn, dtype=jnp.int32)) * cn + my_c
    count = dest.shape[0]
    slots = jnp.arange(count, dtype=jnp.int32)
    idx = jnp.min(jnp.where(target[:, None] == dest[None, :], slots[None, :], count), axis=1)
    send = jnp.take(body, idx, axis=0, mode="fill", fill_value=0)
    send = send.reshape((zh_n, zl_n) + send.shape[1:])
    got = lax.all_to_all(send, "zl", 1, 1, tiled=False)
    part = jnp.sum(got.astype(jnp.float32), axis=1).astype(jnp.bfloat16)
    got = lax.all_to_all(part, "zh", 0, 0, tiled=False)
    return jnp.sum(got.astype(jnp.float32), axis=0).astype(jnp.bfloat16)


def per_device(
    queries,
    forget_logits,
    values,
    gate_input,
    init_states,
    norm_gain,
    out_weight,
    dealing,
    accepted,
):
    local_count = queries.shape[0]
    draft_len = queries.shape[1]
    head_local = init_states.shape[1]
    head_size = init_states.shape[3]
    token_tuple = (queries, forget_logits, values, gate_input)
    got = route_two_stage(token_tuple, dealing)
    hn = lax.axis_size("head")
    partial_out = mixer(got, init_states[0], norm_gain.reshape(1, head_size), out_weight, hn)
    new_states = new_state(accepted, got, init_states[0])[None]
    swapped = lax.all_to_all(partial_out, "head", 0, 0, tiled=True)
    summed = jnp.sum(swapped, axis=0)
    verified = summed.astype(jnp.bfloat16).reshape(local_count, draft_len, summed.shape[1])
    return (verified, new_states)


def solution(mesh):
    xs, cs, zl = 4, 2, 4
    zh = mesh.shape["req"] // (xs * cs * zl)
    sub = Mesh(mesh.devices.reshape(xs, zh, zl, cs, mesh.shape["head"]), ("x", "zh", "zl", "c", "head"))
    placed = (
        P(REQ, None, "head"),
        P(REQ, None, "head"),
        P(REQ, None, "head"),
        P(REQ, None, "head"),
        P(REQ, "head", None, None),
        P(),
        P("head", None),
        P(REQ),
        P(REQ),
    )
    return jax.shard_map(
        per_device,
        mesh=sub,
        in_specs=placed,
        out_specs=(P(REQ, None, "head"), P(REQ, "head", None, None)),
        check_vma=False,
    )
```

```python
import jax
import jax.numpy as jnp
from jax import lax
from jax.experimental import pallas as pl
from jax.experimental.pallas import tpu as pltpu
from jax.sharding import Mesh, PartitionSpec as P

lower_bound = 0.8
norm_eps = 1e-05

ROW = ("x", "c")
REQ = ("x", "zh", "zl", "c")


HI = lax.Precision.HIGHEST


def _dot(a, b):
    return jnp.dot(a, b, precision=HI, preferred_element_type=jnp.float32)


def mixer_kernel(acc_ref, tok_ref, s0_ref, gain_ref, w_hbm, new_ref, part_ref, w_vmem, mixed_scr, sem):
    w_copy = pltpu.make_async_copy(w_hbm, w_vmem, sem)
    w_copy.start()
    acc = acc_ref[0]
    blocks = tok_ref[...].astype(jnp.float32)
    heads = s0_ref.shape[0]
    hd = s0_ref.shape[2]
    width = heads * hd
    q = blocks[:, 0:width]
    fl = blocks[:, width:2 * width]
    v = blocks[:, 2 * width:3 * width]
    g = blocks[:, 3 * width:4 * width]
    t_len = q.shape[0]
    a = lower_bound + (1.0 - lower_bound) * (1.0 / (1.0 + jnp.exp(-fl)))
    b = 1.0 - a
    la = jnp.log(a)
    row = lax.broadcasted_iota(jnp.int32, (t_len, t_len), 0)
    col = lax.broadcasted_iota(jnp.int32, (t_len, t_len), 1)
    causal = (col <= row).astype(jnp.float32)
    lc = _dot(causal, la)
    big_a = jnp.exp(lc)
    inv_a = jnp.exp(-lc)
    qa = q * big_a
    ba = b * inv_a
    kept_t = (lax.broadcasted_iota(jnp.int32, (la.shape[1], t_len), 1) < acc).astype(jnp.float32)
    a_col = jnp.exp(jnp.sum(kept_t * jnp.transpose(la), axis=1, keepdims=True))
    w_t = kept_t * a_col * jnp.transpose(ba)
    gain = gain_ref[...]
    silu_g = g * (1.0 / (1.0 + jnp.exp(-g)))
    for h in range(heads):
        lanes = slice(h * hd, (h + 1) * hd)
        s0 = s0_ref[h]
        v_h = v[:, lanes]
        qa_h = qa[:, lanes]
        scores = lax.dot_general(qa_h, ba[:, lanes], (((1,), (1,)), ((), ())),
                                 precision=HI, preferred_element_type=jnp.float32)
        o_h = _dot(qa_h, s0) + _dot(scores * causal, v_h)
        new_ref[h] = a_col[lanes] * s0 + _dot(w_t[lanes], v_h)
        meansq = jnp.mean(o_h * o_h, axis=-1, keepdims=True)
        mixed = o_h * lax.rsqrt(meansq + norm_eps) * gain * silu_g[:, lanes]
        mixed_scr[:, lanes] = mixed.astype(mixed_scr.dtype)
    w_copy.wait()
    chunk = part_ref.shape[2]
    mixed_all = mixed_scr[...]
    for j in range(part_ref.shape[0]):
        part_ref[j] = jnp.dot(mixed_all, w_vmem[:, j * chunk:(j + 1) * chunk],
                              preferred_element_type=jnp.float32)


def mixer(acc, tok, s0, gain, weight, parts):
    heads, hd = s0.shape[0], s0.shape[2]
    t_len = tok.shape[0]
    vmem = pl.BlockSpec(memory_space=pltpu.VMEM)
    return pl.pallas_call(
        mixer_kernel,
        out_shape=(jax.ShapeDtypeStruct(s0.shape, jnp.float32),
                   jax.ShapeDtypeStruct((parts, t_len, weight.shape[1] // parts), jnp.float32)),
        in_specs=[pl.BlockSpec(memory_space=pltpu.SMEM), vmem, vmem, vmem,
                  pl.BlockSpec(memory_space=pl.ANY)],
        out_specs=(vmem, vmem),
        scratch_shapes=[pltpu.VMEM(weight.shape, weight.dtype),
                        pltpu.VMEM((t_len, heads * hd), jnp.bfloat16),
                        pltpu.SemaphoreType.DMA(())],
    )(acc, tok, s0, gain, weight)


def route_two_stage(token_tuple, dealing):
    rows, width = token_tuple[0].shape[1:]
    wide = width * len(token_tuple)
    total = wide + 128
    lane = lax.broadcasted_iota(jnp.int32, (rows, total), 1)
    payload = jnp.broadcast_to((dealing[0] + 1).astype(jnp.bfloat16), (rows, total))
    for i, t in enumerate(token_tuple):
        placed = jnp.pad(t[0], ((0, 0), (i * width, total - (i + 1) * width)))
        inside = (lane >= i * width) & (lane < (i + 1) * width)
        payload = jnp.where(inside, placed, payload)
    gathered = lax.all_gather(payload, ROW, axis=0, tiled=False)
    dest = gathered[:, 0, wide].astype(jnp.int32) - 1
    body = gathered[:, :, :wide]
    zh_n = lax.axis_size("zh")
    zl_n = lax.axis_size("zl")
    zn = zh_n * zl_n
    my_x = lax.axis_index("x")
    my_c = lax.axis_index("c")
    cn = lax.axis_size("c")
    target = (my_x * zn + jnp.arange(zn, dtype=jnp.int32)) * cn + my_c
    count = dest.shape[0]
    slots = jnp.arange(count, dtype=jnp.int32)
    idx = jnp.min(jnp.where(target[:, None] == dest[None, :], slots[None, :], count), axis=1)
    send = jnp.take(body, idx, axis=0, mode="fill", fill_value=0)
    send = send.reshape((zh_n, zl_n) + send.shape[1:])
    got = lax.all_to_all(send, "zl", 1, 1, tiled=False)
    part = jnp.sum(got.astype(jnp.float32), axis=1).astype(jnp.bfloat16)
    got = lax.all_to_all(part, "zh", 0, 0, tiled=False)
    return jnp.sum(got.astype(jnp.float32), axis=0).astype(jnp.bfloat16)


def per_device(
    queries,
    forget_logits,
    values,
    gate_input,
    init_states,
    norm_gain,
    out_weight,
    dealing,
    accepted,
):
    local_count = queries.shape[0]
    draft_len = queries.shape[1]
    head_local = init_states.shape[1]
    head_size = init_states.shape[3]
    token_tuple = (queries, forget_logits, values, gate_input)
    got = route_two_stage(token_tuple, dealing)
    hn = lax.axis_size("head")
    new_states, partial_out = mixer(accepted, got, init_states[0], norm_gain.reshape(1, head_size), out_weight, hn)
    new_states = new_states[None]
    swapped = lax.all_to_all(partial_out, "head", 0, 0, tiled=True)
    summed = jnp.sum(swapped, axis=0)
    verified = summed.astype(jnp.bfloat16).reshape(local_count, draft_len, summed.shape[1])
    return (verified, new_states)


def solution(mesh):
    xs, cs, zl = 4, 2, 4
    zh = mesh.shape["req"] // (xs * cs * zl)
    sub = Mesh(mesh.devices.reshape(xs, zh, zl, cs, mesh.shape["head"]), ("x", "zh", "zl", "c", "head"))
    placed = (
        P(REQ, None, "head"),
        P(REQ, None, "head"),
        P(REQ, None, "head"),
        P(REQ, None, "head"),
        P(REQ, "head", None, None),
        P(),
        P("head", None),
        P(REQ),
        P(REQ),
    )
    return jax.shard_map(
        per_device,
        mesh=sub,
        in_specs=placed,
        out_specs=(P(REQ, None, "head"), P(REQ, "head", None, None)),
        check_vma=False,
    )
```

```python
import jax
import jax.numpy as jnp
from jax import lax
from jax.experimental import pallas as pl
from jax.experimental.pallas import tpu as pltpu
from jax.sharding import Mesh, PartitionSpec as P

lower_bound = 0.8
norm_eps = 1e-05

ROW = ("x", "c")
REQ = ("x", "zh", "zl", "c")


HI = lax.Precision.HIGH


def _dot(a, b):
    return jnp.dot(a, b, precision=HI, preferred_element_type=jnp.float32)


def mixer_kernel(acc_ref, tok_ref, s0_ref, gain_ref, w_hbm, new_ref, part_ref, w_vmem, mixed_scr, sem):
    w_copy = pltpu.make_async_copy(w_hbm, w_vmem, sem)
    w_copy.start()
    acc = acc_ref[0]
    blocks = tok_ref[...].astype(jnp.float32)
    heads = s0_ref.shape[0]
    hd = s0_ref.shape[2]
    width = heads * hd
    q = blocks[:, 0:width]
    fl = blocks[:, width:2 * width]
    v = blocks[:, 2 * width:3 * width]
    g = blocks[:, 3 * width:4 * width]
    t_len = q.shape[0]
    a = lower_bound + (1.0 - lower_bound) * (1.0 / (1.0 + jnp.exp(-fl)))
    b = 1.0 - a
    la = jnp.log(a)
    row = lax.broadcasted_iota(jnp.int32, (t_len, t_len), 0)
    col = lax.broadcasted_iota(jnp.int32, (t_len, t_len), 1)
    causal = (col <= row).astype(jnp.float32)
    lc = _dot(causal, la)
    big_a = jnp.exp(lc)
    inv_a = jnp.exp(-lc)
    qa = q * big_a
    ba = b * inv_a
    kept_t = (lax.broadcasted_iota(jnp.int32, (la.shape[1], t_len), 1) < acc).astype(jnp.float32)
    a_col = jnp.exp(jnp.sum(kept_t * jnp.transpose(la), axis=1, keepdims=True))
    w_t = kept_t * a_col * jnp.transpose(ba)
    gain = gain_ref[...]
    silu_g = g * (1.0 / (1.0 + jnp.exp(-g)))
    for h in range(heads):
        lanes = slice(h * hd, (h + 1) * hd)
        s0 = s0_ref[h]
        v_h = v[:, lanes]
        qa_h = qa[:, lanes]
        scores = lax.dot_general(qa_h, ba[:, lanes], (((1,), (1,)), ((), ())),
                                 precision=HI, preferred_element_type=jnp.float32)
        o_h = _dot(qa_h, s0) + _dot(scores * causal, v_h)
        new_ref[h] = a_col[lanes] * s0 + _dot(w_t[lanes], v_h)
        meansq = jnp.mean(o_h * o_h, axis=-1, keepdims=True)
        mixed = o_h * lax.rsqrt(meansq + norm_eps) * gain * silu_g[:, lanes]
        mixed_scr[:, lanes] = mixed.astype(mixed_scr.dtype)
    w_copy.wait()
    chunk = part_ref.shape[2]
    mixed_all = mixed_scr[...]
    for j in range(part_ref.shape[0]):
        part_ref[j] = jnp.dot(mixed_all, w_vmem[:, j * chunk:(j + 1) * chunk],
                              preferred_element_type=jnp.float32)


def mixer(acc, tok, s0, gain, weight, parts):
    heads, hd = s0.shape[0], s0.shape[2]
    t_len = tok.shape[0]
    vmem = pl.BlockSpec(memory_space=pltpu.VMEM)
    return pl.pallas_call(
        mixer_kernel,
        out_shape=(jax.ShapeDtypeStruct(s0.shape, jnp.float32),
                   jax.ShapeDtypeStruct((parts, t_len, weight.shape[1] // parts), jnp.float32)),
        in_specs=[pl.BlockSpec(memory_space=pltpu.SMEM), vmem, vmem, vmem,
                  pl.BlockSpec(memory_space=pl.ANY)],
        out_specs=(vmem, vmem),
        scratch_shapes=[pltpu.VMEM(weight.shape, weight.dtype),
                        pltpu.VMEM((t_len, heads * hd), jnp.bfloat16),
                        pltpu.SemaphoreType.DMA(())],
    )(acc, tok, s0, gain, weight)


def route_two_stage(token_tuple, dealing):
    rows, width = token_tuple[0].shape[1:]
    wide = width * len(token_tuple)
    total = wide + 128
    lane = lax.broadcasted_iota(jnp.int32, (rows, total), 1)
    payload = jnp.broadcast_to((dealing[0] + 1).astype(jnp.bfloat16), (rows, total))
    for i, t in enumerate(token_tuple):
        placed = jnp.pad(t[0], ((0, 0), (i * width, total - (i + 1) * width)))
        inside = (lane >= i * width) & (lane < (i + 1) * width)
        payload = jnp.where(inside, placed, payload)
    gathered = lax.all_gather(payload, ROW, axis=0, tiled=False)
    dest = gathered[:, 0, wide].astype(jnp.int32) - 1
    body = gathered[:, :, :wide]
    zh_n = lax.axis_size("zh")
    zl_n = lax.axis_size("zl")
    zn = zh_n * zl_n
    my_x = lax.axis_index("x")
    my_c = lax.axis_index("c")
    cn = lax.axis_size("c")
    target = (my_x * zn + jnp.arange(zn, dtype=jnp.int32)) * cn + my_c
    count = dest.shape[0]
    slots = jnp.arange(count, dtype=jnp.int32)
    idx = jnp.min(jnp.where(target[:, None] == dest[None, :], slots[None, :], count), axis=1)
    send = jnp.take(body, idx, axis=0, mode="fill", fill_value=0)
    send = send.reshape((zh_n, zl_n) + send.shape[1:])
    got = lax.all_to_all(send, "zl", 1, 1, tiled=False)
    part = jnp.sum(got.astype(jnp.float32), axis=1).astype(jnp.bfloat16)
    got = lax.all_to_all(part, "zh", 0, 0, tiled=False)
    return jnp.sum(got.astype(jnp.float32), axis=0).astype(jnp.bfloat16)


def per_device(
    queries,
    forget_logits,
    values,
    gate_input,
    init_states,
    norm_gain,
    out_weight,
    dealing,
    accepted,
):
    local_count = queries.shape[0]
    draft_len = queries.shape[1]
    head_local = init_states.shape[1]
    head_size = init_states.shape[3]
    token_tuple = (queries, forget_logits, values, gate_input)
    got = route_two_stage(token_tuple, dealing)
    hn = lax.axis_size("head")
    new_states, partial_out = mixer(accepted, got, init_states[0], norm_gain.reshape(1, head_size), out_weight, hn)
    new_states = new_states[None]
    swapped = lax.all_to_all(partial_out, "head", 0, 0, tiled=True)
    summed = jnp.sum(swapped, axis=0)
    verified = summed.astype(jnp.bfloat16).reshape(local_count, draft_len, summed.shape[1])
    return (verified, new_states)


def solution(mesh):
    xs, cs, zl = 4, 2, 4
    zh = mesh.shape["req"] // (xs * cs * zl)
    sub = Mesh(mesh.devices.reshape(xs, zh, zl, cs, mesh.shape["head"]), ("x", "zh", "zl", "c", "head"))
    placed = (
        P(REQ, None, "head"),
        P(REQ, None, "head"),
        P(REQ, None, "head"),
        P(REQ, None, "head"),
        P(REQ, "head", None, None),
        P(),
        P("head", None),
        P(REQ),
        P(REQ),
    )
    return jax.shard_map(
        per_device,
        mesh=sub,
        in_specs=placed,
        out_specs=(P(REQ, None, "head"), P(REQ, "head", None, None)),
        check_vma=False,
    )
```

```python
import jax
import jax.numpy as jnp
from jax import lax
from jax.experimental import pallas as pl
from jax.experimental.pallas import tpu as pltpu
from jax.sharding import Mesh, PartitionSpec as P

lower_bound = 0.8
norm_eps = 1e-05

ROW = ("x", "c")
REQ = ("x", "zh", "zl", "c")


HI = lax.Precision.HIGHEST


def _dot(a, b):
    return jnp.dot(a, b, precision=HI, preferred_element_type=jnp.float32)


def mixer_kernel(acc_ref, tok_ref, s0_ref, gain_ref, w_hbm, new_ref, part_ref, w_vmem, mixed_scr, sem):
    pieces = sem.shape[0]
    step = w_hbm.shape[0] // pieces
    w_copies = []
    for j in range(pieces):
        rows = pl.ds(j * step, step)
        w_copies.append(pltpu.make_async_copy(w_hbm.at[rows], w_vmem.at[rows], sem.at[j]))
        w_copies[-1].start()
    acc = acc_ref[0]
    blocks = tok_ref[...].astype(jnp.float32)
    heads = s0_ref.shape[0]
    hd = s0_ref.shape[2]
    width = heads * hd
    q = blocks[:, 0:width]
    fl = blocks[:, width:2 * width]
    v = blocks[:, 2 * width:3 * width]
    g = blocks[:, 3 * width:4 * width]
    t_len = q.shape[0]
    a = lower_bound + (1.0 - lower_bound) * (1.0 / (1.0 + jnp.exp(-fl)))
    b = 1.0 - a
    la = jnp.log(a)
    row = lax.broadcasted_iota(jnp.int32, (t_len, t_len), 0)
    col = lax.broadcasted_iota(jnp.int32, (t_len, t_len), 1)
    causal = (col <= row).astype(jnp.float32)
    lc = _dot(causal, la)
    big_a = jnp.exp(lc)
    inv_a = jnp.exp(-lc)
    qa = q * big_a
    ba = b * inv_a
    kept_t = (lax.broadcasted_iota(jnp.int32, (la.shape[1], t_len), 1) < acc).astype(jnp.float32)
    a_col = jnp.exp(jnp.sum(kept_t * jnp.transpose(la), axis=1, keepdims=True))
    w_t = kept_t * a_col * jnp.transpose(ba)
    gain = gain_ref[...]
    silu_g = g * (1.0 / (1.0 + jnp.exp(-g)))
    for h in range(heads):
        lanes = slice(h * hd, (h + 1) * hd)
        s0 = s0_ref[h]
        v_h = v[:, lanes]
        qa_h = qa[:, lanes]
        scores = lax.dot_general(qa_h, ba[:, lanes], (((1,), (1,)), ((), ())),
                                 precision=HI, preferred_element_type=jnp.float32)
        o_h = _dot(qa_h, s0) + _dot(scores * causal, v_h)
        new_ref[h] = a_col[lanes] * s0 + _dot(w_t[lanes], v_h)
        meansq = jnp.mean(o_h * o_h, axis=-1, keepdims=True)
        mixed = o_h * lax.rsqrt(meansq + norm_eps) * gain * silu_g[:, lanes]
        mixed_scr[:, lanes] = mixed.astype(mixed_scr.dtype)
    for w_copy in w_copies:
        w_copy.wait()
    chunk = part_ref.shape[2]
    mixed_all = mixed_scr[...]
    for j in range(part_ref.shape[0]):
        part_ref[j] = jnp.dot(mixed_all, w_vmem[:, j * chunk:(j + 1) * chunk],
                              preferred_element_type=jnp.float32)


def mixer(acc, tok, s0, gain, weight, parts):
    heads, hd = s0.shape[0], s0.shape[2]
    t_len = tok.shape[0]
    vmem = pl.BlockSpec(memory_space=pltpu.VMEM)
    return pl.pallas_call(
        mixer_kernel,
        out_shape=(jax.ShapeDtypeStruct(s0.shape, jnp.float32),
                   jax.ShapeDtypeStruct((parts, t_len, weight.shape[1] // parts), jnp.float32)),
        in_specs=[pl.BlockSpec(memory_space=pltpu.SMEM), vmem, vmem, vmem,
                  pl.BlockSpec(memory_space=pl.ANY)],
        out_specs=(vmem, vmem),
        scratch_shapes=[pltpu.VMEM(weight.shape, weight.dtype),
                        pltpu.VMEM((t_len, heads * hd), jnp.bfloat16),
                        pltpu.SemaphoreType.DMA((4,))],
    )(acc, tok, s0, gain, weight)


def route_two_stage(token_tuple, dealing):
    rows, width = token_tuple[0].shape[1:]
    wide = width * len(token_tuple)
    total = wide + 128
    lane = lax.broadcasted_iota(jnp.int32, (rows, total), 1)
    payload = jnp.broadcast_to((dealing[0] + 1).astype(jnp.bfloat16), (rows, total))
    for i, t in enumerate(token_tuple):
        placed = jnp.pad(t[0], ((0, 0), (i * width, total - (i + 1) * width)))
        inside = (lane >= i * width) & (lane < (i + 1) * width)
        payload = jnp.where(inside, placed, payload)
    gathered = lax.all_gather(payload, ROW, axis=0, tiled=False)
    dest = gathered[:, 0, wide].astype(jnp.int32) - 1
    body = gathered[:, :, :wide]
    zh_n = lax.axis_size("zh")
    zl_n = lax.axis_size("zl")
    zn = zh_n * zl_n
    my_x = lax.axis_index("x")
    my_c = lax.axis_index("c")
    cn = lax.axis_size("c")
    target = (my_x * zn + jnp.arange(zn, dtype=jnp.int32)) * cn + my_c
    count = dest.shape[0]
    slots = jnp.arange(count, dtype=jnp.int32)
    idx = jnp.min(jnp.where(target[:, None] == dest[None, :], slots[None, :], count), axis=1)
    send = jnp.take(body, idx, axis=0, mode="fill", fill_value=0)
    send = send.reshape((zh_n, zl_n) + send.shape[1:])
    got = lax.all_to_all(send, "zl", 1, 1, tiled=False)
    part = jnp.sum(got.astype(jnp.float32), axis=1).astype(jnp.bfloat16)
    got = lax.all_to_all(part, "zh", 0, 0, tiled=False)
    return jnp.sum(got.astype(jnp.float32), axis=0).astype(jnp.bfloat16)


def per_device(
    queries,
    forget_logits,
    values,
    gate_input,
    init_states,
    norm_gain,
    out_weight,
    dealing,
    accepted,
):
    local_count = queries.shape[0]
    draft_len = queries.shape[1]
    head_local = init_states.shape[1]
    head_size = init_states.shape[3]
    token_tuple = (queries, forget_logits, values, gate_input)
    got = route_two_stage(token_tuple, dealing)
    hn = lax.axis_size("head")
    new_states, partial_out = mixer(accepted, got, init_states[0], norm_gain.reshape(1, head_size), out_weight, hn)
    new_states = new_states[None]
    swapped = lax.all_to_all(partial_out, "head", 0, 0, tiled=True)
    summed = jnp.sum(swapped, axis=0)
    verified = summed.astype(jnp.bfloat16).reshape(local_count, draft_len, summed.shape[1])
    return (verified, new_states)


def solution(mesh):
    xs, cs, zl = 4, 2, 4
    zh = mesh.shape["req"] // (xs * cs * zl)
    sub = Mesh(mesh.devices.reshape(xs, zh, zl, cs, mesh.shape["head"]), ("x", "zh", "zl", "c", "head"))
    placed = (
        P(REQ, None, "head"),
        P(REQ, None, "head"),
        P(REQ, None, "head"),
        P(REQ, None, "head"),
        P(REQ, "head", None, None),
        P(),
        P("head", None),
        P(REQ),
        P(REQ),
    )
    return jax.shard_map(
        per_device,
        mesh=sub,
        in_specs=placed,
        out_specs=(P(REQ, None, "head"), P(REQ, "head", None, None)),
        check_vma=False,
    )
```

```python
import jax
import jax.numpy as jnp
from jax import lax
from jax.experimental import pallas as pl
from jax.experimental.pallas import tpu as pltpu
from jax.sharding import Mesh, PartitionSpec as P

lower_bound = 0.8
norm_eps = 1e-05

ROW = ("x", "c")
REQ = ("x", "zh", "zl", "c")


HI = lax.Precision.HIGHEST


def _dot(a, b):
    return jnp.dot(a, b, precision=HI, preferred_element_type=jnp.float32)


def mixer_kernel(acc_ref, tok_ref, s0_hbm, gain_ref, w_hbm, new_hbm, part_ref,
                 w_vmem, mixed_scr, s0_ref, new_ref, sem, s0_sem, new_sem):
    pieces = sem.shape[0]
    step = w_hbm.shape[0] // pieces
    w_copies = []
    for j in range(pieces):
        rows = pl.ds(j * step, step)
        w_copies.append(pltpu.make_async_copy(w_hbm.at[rows], w_vmem.at[rows], sem.at[j]))
        w_copies[-1].start()
    s0_copies = [pltpu.make_async_copy(s0_hbm.at[h], s0_ref.at[h], s0_sem.at[h])
                 for h in range(s0_ref.shape[0])]
    for copy in s0_copies:
        copy.start()
    acc = acc_ref[0]
    blocks = tok_ref[...].astype(jnp.float32)
    heads = s0_ref.shape[0]
    hd = s0_ref.shape[2]
    width = heads * hd
    q = blocks[:, 0:width]
    fl = blocks[:, width:2 * width]
    v = blocks[:, 2 * width:3 * width]
    g = blocks[:, 3 * width:4 * width]
    t_len = q.shape[0]
    a = lower_bound + (1.0 - lower_bound) * (1.0 / (1.0 + jnp.exp(-fl)))
    b = 1.0 - a
    la = jnp.log(a)
    row = lax.broadcasted_iota(jnp.int32, (t_len, t_len), 0)
    col = lax.broadcasted_iota(jnp.int32, (t_len, t_len), 1)
    causal = (col <= row).astype(jnp.float32)
    lc = _dot(causal, la)
    big_a = jnp.exp(lc)
    inv_a = jnp.exp(-lc)
    qa = q * big_a
    ba = b * inv_a
    kept_t = (lax.broadcasted_iota(jnp.int32, (la.shape[1], t_len), 1) < acc).astype(jnp.float32)
    a_col = jnp.exp(jnp.sum(kept_t * jnp.transpose(la), axis=1, keepdims=True))
    w_t = kept_t * a_col * jnp.transpose(ba)
    gain = gain_ref[...]
    silu_g = g * (1.0 / (1.0 + jnp.exp(-g)))
    new_copies = []
    for h in range(heads):
        lanes = slice(h * hd, (h + 1) * hd)
        s0_copies[h].wait()
        s0 = s0_ref[h]
        v_h = v[:, lanes]
        qa_h = qa[:, lanes]
        scores = lax.dot_general(qa_h, ba[:, lanes], (((1,), (1,)), ((), ())),
                                 precision=HI, preferred_element_type=jnp.float32)
        o_h = _dot(qa_h, s0) + _dot(scores * causal, v_h)
        new_ref[h] = a_col[lanes] * s0 + _dot(w_t[lanes], v_h)
        new_copies.append(pltpu.make_async_copy(new_ref.at[h], new_hbm.at[h], new_sem.at[h]))
        new_copies[-1].start()
        meansq = jnp.mean(o_h * o_h, axis=-1, keepdims=True)
        mixed = o_h * lax.rsqrt(meansq + norm_eps) * gain * silu_g[:, lanes]
        mixed_scr[:, lanes] = mixed.astype(mixed_scr.dtype)
    for w_copy in w_copies:
        w_copy.wait()
    chunk = part_ref.shape[2]
    mixed_all = mixed_scr[...]
    for j in range(part_ref.shape[0]):
        part_ref[j] = jnp.dot(mixed_all, w_vmem[:, j * chunk:(j + 1) * chunk],
                              preferred_element_type=jnp.float32)
    for copy in new_copies:
        copy.wait()


def mixer(acc, tok, s0, gain, weight, parts):
    heads, hd = s0.shape[0], s0.shape[2]
    t_len = tok.shape[0]
    vmem = pl.BlockSpec(memory_space=pltpu.VMEM)
    anywhere = pl.BlockSpec(memory_space=pl.ANY)
    return pl.pallas_call(
        mixer_kernel,
        out_shape=(jax.ShapeDtypeStruct(s0.shape, jnp.float32),
                   jax.ShapeDtypeStruct((parts, t_len, weight.shape[1] // parts), jnp.float32)),
        in_specs=[pl.BlockSpec(memory_space=pltpu.SMEM), vmem, anywhere, vmem, anywhere],
        out_specs=(anywhere, vmem),
        scratch_shapes=[pltpu.VMEM(weight.shape, weight.dtype),
                        pltpu.VMEM((t_len, heads * hd), jnp.bfloat16),
                        pltpu.VMEM(s0.shape, jnp.float32),
                        pltpu.VMEM(s0.shape, jnp.float32),
                        pltpu.SemaphoreType.DMA((4,)),
                        pltpu.SemaphoreType.DMA((heads,)),
                        pltpu.SemaphoreType.DMA((heads,))],
    )(acc, tok, s0, gain, weight)


def route_two_stage(token_tuple, dealing):
    rows, width = token_tuple[0].shape[1:]
    wide = width * len(token_tuple)
    total = wide + 128
    lane = lax.broadcasted_iota(jnp.int32, (rows, total), 1)
    payload = jnp.broadcast_to((dealing[0] + 1).astype(jnp.bfloat16), (rows, total))
    for i, t in enumerate(token_tuple):
        placed = jnp.pad(t[0], ((0, 0), (i * width, total - (i + 1) * width)))
        inside = (lane >= i * width) & (lane < (i + 1) * width)
        payload = jnp.where(inside, placed, payload)
    gathered = lax.all_gather(payload, ROW, axis=0, tiled=False)
    dest = gathered[:, 0, wide].astype(jnp.int32) - 1
    body = gathered[:, :, :wide]
    zh_n = lax.axis_size("zh")
    zl_n = lax.axis_size("zl")
    zn = zh_n * zl_n
    my_x = lax.axis_index("x")
    my_c = lax.axis_index("c")
    cn = lax.axis_size("c")
    target = (my_x * zn + jnp.arange(zn, dtype=jnp.int32)) * cn + my_c
    count = dest.shape[0]
    slots = jnp.arange(count, dtype=jnp.int32)
    idx = jnp.min(jnp.where(target[:, None] == dest[None, :], slots[None, :], count), axis=1)
    send = jnp.take(body, idx, axis=0, mode="fill", fill_value=0)
    send = send.reshape((zh_n, zl_n) + send.shape[1:])
    got = lax.all_to_all(send, "zl", 1, 1, tiled=False)
    part = jnp.sum(got.astype(jnp.float32), axis=1).astype(jnp.bfloat16)
    got = lax.all_to_all(part, "zh", 0, 0, tiled=False)
    return jnp.sum(got.astype(jnp.float32), axis=0).astype(jnp.bfloat16)


def per_device(
    queries,
    forget_logits,
    values,
    gate_input,
    init_states,
    norm_gain,
    out_weight,
    dealing,
    accepted,
):
    local_count = queries.shape[0]
    draft_len = queries.shape[1]
    head_local = init_states.shape[1]
    head_size = init_states.shape[3]
    token_tuple = (queries, forget_logits, values, gate_input)
    got = route_two_stage(token_tuple, dealing)
    hn = lax.axis_size("head")
    new_states, partial_out = mixer(accepted, got, init_states[0], norm_gain.reshape(1, head_size), out_weight, hn)
    new_states = new_states[None]
    swapped = lax.all_to_all(partial_out, "head", 0, 0, tiled=True)
    summed = jnp.sum(swapped, axis=0)
    verified = summed.astype(jnp.bfloat16).reshape(local_count, draft_len, summed.shape[1])
    return (verified, new_states)


def solution(mesh):
    xs, cs, zl = 4, 2, 4
    zh = mesh.shape["req"] // (xs * cs * zl)
    sub = Mesh(mesh.devices.reshape(xs, zh, zl, cs, mesh.shape["head"]), ("x", "zh", "zl", "c", "head"))
    placed = (
        P(REQ, None, "head"),
        P(REQ, None, "head"),
        P(REQ, None, "head"),
        P(REQ, None, "head"),
        P(REQ, "head", None, None),
        P(),
        P("head", None),
        P(REQ),
        P(REQ),
    )
    return jax.shard_map(
        per_device,
        mesh=sub,
        in_specs=placed,
        out_specs=(P(REQ, None, "head"), P(REQ, "head", None, None)),
        check_vma=False,
    )
```

```python
import jax
import jax.numpy as jnp
from jax import lax
from jax.experimental import pallas as pl
from jax.experimental.pallas import tpu as pltpu
from jax.sharding import Mesh, PartitionSpec as P

lower_bound = 0.8
norm_eps = 1e-05

ROW = ("x", "c")
REQ = ("x", "zh", "zl", "c")


HI = lax.Precision.HIGHEST


def _dot(a, b):
    return jnp.dot(a, b, precision=HI, preferred_element_type=jnp.float32)


def mixer_kernel(acc_ref, tok_ref, s0_ref, gain_ref, w_hbm, new_ref, part_ref, w_vmem, mixed_scr, sem):
    pieces = sem.shape[0]
    step = w_hbm.shape[0] // pieces
    w_copies = []
    for j in range(pieces):
        rows = pl.ds(j * step, step)
        w_copies.append(pltpu.make_async_copy(w_hbm.at[rows], w_vmem.at[rows], sem.at[j]))
        w_copies[-1].start()
    acc = acc_ref[0]
    blocks = tok_ref[...].astype(jnp.float32)
    heads = s0_ref.shape[0]
    hd = s0_ref.shape[2]
    width = heads * hd
    q = blocks[:, 0:width]
    fl = blocks[:, width:2 * width]
    v = blocks[:, 2 * width:3 * width]
    g = blocks[:, 3 * width:4 * width]
    t_len = q.shape[0]
    a = lower_bound + (1.0 - lower_bound) * (1.0 / (1.0 + jnp.exp(-fl)))
    b = 1.0 - a
    la = jnp.log(a)
    row = lax.broadcasted_iota(jnp.int32, (t_len, t_len), 0)
    col = lax.broadcasted_iota(jnp.int32, (t_len, t_len), 1)
    causal = (col <= row).astype(jnp.float32)
    lc = _dot(causal, la)
    big_a = jnp.exp(lc)
    inv_a = jnp.exp(-lc)
    qa = q * big_a
    ba = b * inv_a
    kept_t = (lax.broadcasted_iota(jnp.int32, (la.shape[1], t_len), 1) < acc).astype(jnp.float32)
    a_col = jnp.exp(jnp.sum(kept_t * jnp.transpose(la), axis=1, keepdims=True))
    w_t = kept_t * a_col * jnp.transpose(ba)
    gain = gain_ref[...]
    silu_g = g * (1.0 / (1.0 + jnp.exp(-g)))
    for h in range(heads):
        lanes = slice(h * hd, (h + 1) * hd)
        s0 = s0_ref[h]
        v_h = v[:, lanes]
        qa_h = qa[:, lanes]
        scores = lax.dot_general(qa_h, ba[:, lanes], (((1,), (1,)), ((), ())),
                                 precision=HI, preferred_element_type=jnp.float32)
        o_h = _dot(qa_h, s0) + _dot(scores * causal, v_h)
        new_ref[h] = a_col[lanes] * s0 + _dot(w_t[lanes], v_h)
        meansq = jnp.mean(o_h * o_h, axis=-1, keepdims=True)
        mixed = o_h * lax.rsqrt(meansq + norm_eps) * gain * silu_g[:, lanes]
        mixed_scr[:, lanes] = mixed.astype(mixed_scr.dtype)
    for w_copy in w_copies:
        w_copy.wait()
    chunk = part_ref.shape[2]
    mixed_all = mixed_scr[...]
    for j in range(part_ref.shape[0]):
        part_ref[j] = jnp.dot(mixed_all, w_vmem[:, j * chunk:(j + 1) * chunk],
                              preferred_element_type=jnp.float32)


def mixer(acc, tok, s0, gain, weight, parts):
    heads, hd = s0.shape[0], s0.shape[2]
    t_len = tok.shape[0]
    vmem = pl.BlockSpec(memory_space=pltpu.VMEM)
    return pl.pallas_call(
        mixer_kernel,
        out_shape=(jax.ShapeDtypeStruct(s0.shape, jnp.float32),
                   jax.ShapeDtypeStruct((parts, t_len, weight.shape[1] // parts), jnp.float32)),
        in_specs=[pl.BlockSpec(memory_space=pltpu.SMEM), vmem, vmem, vmem,
                  pl.BlockSpec(memory_space=pl.ANY)],
        out_specs=(vmem, vmem),
        scratch_shapes=[pltpu.VMEM(weight.shape, weight.dtype),
                        pltpu.VMEM((t_len, heads * hd), jnp.bfloat16),
                        pltpu.SemaphoreType.DMA((4,))],
    )(acc, tok, s0, gain, weight)


def route_two_stage(token_tuple, dealing):
    rows, width = token_tuple[0].shape[1:]
    wide = width * len(token_tuple)
    total = wide + 128
    lane = lax.broadcasted_iota(jnp.int32, (rows, total), 1)
    payload = jnp.broadcast_to((dealing[0] + 1).astype(jnp.bfloat16), (rows, total))
    for i, t in enumerate(token_tuple):
        placed = jnp.pad(t[0], ((0, 0), (i * width, total - (i + 1) * width)))
        inside = (lane >= i * width) & (lane < (i + 1) * width)
        payload = jnp.where(inside, placed, payload)
    zn_all = lax.axis_size("zh") * lax.axis_size("zl")
    cn_all = lax.axis_size("c")
    dest_col = (dealing[0] // (zn_all * cn_all)) * cn_all + dealing[0] % cn_all
    group = lax.axis_size("x") * cn_all
    pick = (jnp.arange(group, dtype=jnp.int32) == dest_col)[:, None, None]
    send1 = jnp.where(pick, payload[None], jnp.zeros_like(payload)[None])
    gathered = lax.all_to_all(send1, ROW, 0, 0, tiled=False)
    dest = gathered[:, 0, wide].astype(jnp.int32) - 1
    body = gathered[:, :, :wide]
    zh_n = lax.axis_size("zh")
    zl_n = lax.axis_size("zl")
    zn = zh_n * zl_n
    my_x = lax.axis_index("x")
    my_c = lax.axis_index("c")
    cn = lax.axis_size("c")
    target = (my_x * zn + jnp.arange(zn, dtype=jnp.int32)) * cn + my_c
    count = dest.shape[0]
    slots = jnp.arange(count, dtype=jnp.int32)
    idx = jnp.min(jnp.where(target[:, None] == dest[None, :], slots[None, :], count), axis=1)
    send = jnp.take(body, idx, axis=0, mode="fill", fill_value=0)
    send = send.reshape((zh_n, zl_n) + send.shape[1:])
    got = lax.all_to_all(send, "zl", 1, 1, tiled=False)
    part = jnp.sum(got.astype(jnp.float32), axis=1).astype(jnp.bfloat16)
    got = lax.all_to_all(part, "zh", 0, 0, tiled=False)
    return jnp.sum(got.astype(jnp.float32), axis=0).astype(jnp.bfloat16)


def per_device(
    queries,
    forget_logits,
    values,
    gate_input,
    init_states,
    norm_gain,
    out_weight,
    dealing,
    accepted,
):
    local_count = queries.shape[0]
    draft_len = queries.shape[1]
    head_local = init_states.shape[1]
    head_size = init_states.shape[3]
    token_tuple = (queries, forget_logits, values, gate_input)
    got = route_two_stage(token_tuple, dealing)
    hn = lax.axis_size("head")
    new_states, partial_out = mixer(accepted, got, init_states[0], norm_gain.reshape(1, head_size), out_weight, hn)
    new_states = new_states[None]
    swapped = lax.all_to_all(partial_out, "head", 0, 0, tiled=True)
    summed = jnp.sum(swapped, axis=0)
    verified = summed.astype(jnp.bfloat16).reshape(local_count, draft_len, summed.shape[1])
    return (verified, new_states)


def solution(mesh):
    xs, cs, zl = 4, 2, 4
    zh = mesh.shape["req"] // (xs * cs * zl)
    sub = Mesh(mesh.devices.reshape(xs, zh, zl, cs, mesh.shape["head"]), ("x", "zh", "zl", "c", "head"))
    placed = (
        P(REQ, None, "head"),
        P(REQ, None, "head"),
        P(REQ, None, "head"),
        P(REQ, None, "head"),
        P(REQ, "head", None, None),
        P(),
        P("head", None),
        P(REQ),
        P(REQ),
    )
    return jax.shard_map(
        per_device,
        mesh=sub,
        in_specs=placed,
        out_specs=(P(REQ, None, "head"), P(REQ, "head", None, None)),
        check_vma=False,
    )
```

```python
import jax
import jax.numpy as jnp
from jax import lax
from jax.experimental import pallas as pl
from jax.experimental.pallas import tpu as pltpu
from jax.sharding import Mesh, PartitionSpec as P

lower_bound = 0.8
norm_eps = 1e-05

ROW = ("zl", "c")
REQ = ("x", "zh", "zl", "c")


HI = lax.Precision.HIGHEST


def _dot(a, b):
    return jnp.dot(a, b, precision=HI, preferred_element_type=jnp.float32)


def mixer_kernel(acc_ref, tok_ref, s0_ref, gain_ref, w_hbm, new_ref, part_ref, w_vmem, mixed_scr, sem):
    pieces = sem.shape[0]
    step = w_hbm.shape[0] // pieces
    w_copies = []
    for j in range(pieces):
        rows = pl.ds(j * step, step)
        w_copies.append(pltpu.make_async_copy(w_hbm.at[rows], w_vmem.at[rows], sem.at[j]))
        w_copies[-1].start()
    acc = acc_ref[0]
    blocks = tok_ref[...].astype(jnp.float32)
    heads = s0_ref.shape[0]
    hd = s0_ref.shape[2]
    width = heads * hd
    q = blocks[:, 0:width]
    fl = blocks[:, width:2 * width]
    v = blocks[:, 2 * width:3 * width]
    g = blocks[:, 3 * width:4 * width]
    t_len = q.shape[0]
    a = lower_bound + (1.0 - lower_bound) * (1.0 / (1.0 + jnp.exp(-fl)))
    b = 1.0 - a
    la = jnp.log(a)
    row = lax.broadcasted_iota(jnp.int32, (t_len, t_len), 0)
    col = lax.broadcasted_iota(jnp.int32, (t_len, t_len), 1)
    causal = (col <= row).astype(jnp.float32)
    lc = _dot(causal, la)
    big_a = jnp.exp(lc)
    inv_a = jnp.exp(-lc)
    qa = q * big_a
    ba = b * inv_a
    kept_t = (lax.broadcasted_iota(jnp.int32, (la.shape[1], t_len), 1) < acc).astype(jnp.float32)
    a_col = jnp.exp(jnp.sum(kept_t * jnp.transpose(la), axis=1, keepdims=True))
    w_t = kept_t * a_col * jnp.transpose(ba)
    gain = gain_ref[...]
    silu_g = g * (1.0 / (1.0 + jnp.exp(-g)))
    for h in range(heads):
        lanes = slice(h * hd, (h + 1) * hd)
        s0 = s0_ref[h]
        v_h = v[:, lanes]
        qa_h = qa[:, lanes]
        scores = lax.dot_general(qa_h, ba[:, lanes], (((1,), (1,)), ((), ())),
                                 precision=HI, preferred_element_type=jnp.float32)
        o_h = _dot(qa_h, s0) + _dot(scores * causal, v_h)
        new_ref[h] = a_col[lanes] * s0 + _dot(w_t[lanes], v_h)
        meansq = jnp.mean(o_h * o_h, axis=-1, keepdims=True)
        mixed = o_h * lax.rsqrt(meansq + norm_eps) * gain * silu_g[:, lanes]
        mixed_scr[:, lanes] = mixed.astype(mixed_scr.dtype)
    for w_copy in w_copies:
        w_copy.wait()
    chunk = part_ref.shape[2]
    mixed_all = mixed_scr[...]
    for j in range(part_ref.shape[0]):
        part_ref[j] = jnp.dot(mixed_all, w_vmem[:, j * chunk:(j + 1) * chunk],
                              preferred_element_type=jnp.float32)


def mixer(acc, tok, s0, gain, weight, parts):
    heads, hd = s0.shape[0], s0.shape[2]
    t_len = tok.shape[0]
    vmem = pl.BlockSpec(memory_space=pltpu.VMEM)
    return pl.pallas_call(
        mixer_kernel,
        out_shape=(jax.ShapeDtypeStruct(s0.shape, jnp.float32),
                   jax.ShapeDtypeStruct((parts, t_len, weight.shape[1] // parts), jnp.float32)),
        in_specs=[pl.BlockSpec(memory_space=pltpu.SMEM), vmem, vmem, vmem,
                  pl.BlockSpec(memory_space=pl.ANY)],
        out_specs=(vmem, vmem),
        scratch_shapes=[pltpu.VMEM(weight.shape, weight.dtype),
                        pltpu.VMEM((t_len, heads * hd), jnp.bfloat16),
                        pltpu.SemaphoreType.DMA((4,))],
    )(acc, tok, s0, gain, weight)


def route_two_stage(token_tuple, dealing):
    rows, width = token_tuple[0].shape[1:]
    wide = width * len(token_tuple)
    total = wide + 128
    lane = lax.broadcasted_iota(jnp.int32, (rows, total), 1)
    payload = jnp.broadcast_to((dealing[0] + 1).astype(jnp.bfloat16), (rows, total))
    for i, t in enumerate(token_tuple):
        placed = jnp.pad(t[0], ((0, 0), (i * width, total - (i + 1) * width)))
        inside = (lane >= i * width) & (lane < (i + 1) * width)
        payload = jnp.where(inside, placed, payload)
    gathered = lax.all_gather(payload, ROW, axis=0, tiled=False)
    dest = gathered[:, 0, wide].astype(jnp.int32) - 1
    body = gathered[:, :, :wide]
    xn = lax.axis_size("x")
    zh_n = lax.axis_size("zh")
    zl_n = lax.axis_size("zl")
    cn = lax.axis_size("c")
    my_zl = lax.axis_index("zl")
    my_c = lax.axis_index("c")
    xs = jnp.arange(xn, dtype=jnp.int32)[:, None]
    zhs = jnp.arange(zh_n, dtype=jnp.int32)[None, :]
    target = (((xs * zh_n + zhs) * zl_n + my_zl) * cn + my_c).reshape(-1)
    count = dest.shape[0]
    slots = jnp.arange(count, dtype=jnp.int32)
    idx = jnp.min(jnp.where(target[:, None] == dest[None, :], slots[None, :], count), axis=1)
    send = jnp.take(body, idx, axis=0, mode="fill", fill_value=0)
    send = send.reshape((xn, zh_n) + send.shape[1:])
    got = lax.all_to_all(send, "x", 0, 0, tiled=False)
    part = jnp.sum(got.astype(jnp.float32), axis=0).astype(jnp.bfloat16)
    got = lax.all_to_all(part, "zh", 0, 0, tiled=False)
    return jnp.sum(got.astype(jnp.float32), axis=0).astype(jnp.bfloat16)


def per_device(
    queries,
    forget_logits,
    values,
    gate_input,
    init_states,
    norm_gain,
    out_weight,
    dealing,
    accepted,
):
    local_count = queries.shape[0]
    draft_len = queries.shape[1]
    head_local = init_states.shape[1]
    head_size = init_states.shape[3]
    token_tuple = (queries, forget_logits, values, gate_input)
    got = route_two_stage(token_tuple, dealing)
    hn = lax.axis_size("head")
    new_states, partial_out = mixer(accepted, got, init_states[0], norm_gain.reshape(1, head_size), out_weight, hn)
    new_states = new_states[None]
    swapped = lax.all_to_all(partial_out, "head", 0, 0, tiled=True)
    summed = jnp.sum(swapped, axis=0)
    verified = summed.astype(jnp.bfloat16).reshape(local_count, draft_len, summed.shape[1])
    return (verified, new_states)


def solution(mesh):
    xs, cs, zl = 4, 2, 4
    zh = mesh.shape["req"] // (xs * cs * zl)
    sub = Mesh(mesh.devices.reshape(xs, zh, zl, cs, mesh.shape["head"]), ("x", "zh", "zl", "c", "head"))
    placed = (
        P(REQ, None, "head"),
        P(REQ, None, "head"),
        P(REQ, None, "head"),
        P(REQ, None, "head"),
        P(REQ, "head", None, None),
        P(),
        P("head", None),
        P(REQ),
        P(REQ),
    )
    return jax.shard_map(
        per_device,
        mesh=sub,
        in_specs=placed,
        out_specs=(P(REQ, None, "head"), P(REQ, "head", None, None)),
        check_vma=False,
    )
```

```python
import jax
import jax.numpy as jnp
from jax import lax
from jax.experimental import pallas as pl
from jax.experimental.pallas import tpu as pltpu
from jax.sharding import Mesh, PartitionSpec as P

lower_bound = 0.8
norm_eps = 1e-05

ROW = ("zh", "c")
REQ = ("x", "zh", "zl", "c")


HI = lax.Precision.HIGHEST


def _dot(a, b):
    return jnp.dot(a, b, precision=HI, preferred_element_type=jnp.float32)


def mixer_kernel(acc_ref, tok_ref, s0_ref, gain_ref, w_hbm, new_ref, part_ref, w_vmem, mixed_scr, sem):
    pieces = sem.shape[0]
    step = w_hbm.shape[0] // pieces
    w_copies = []
    for j in range(pieces):
        rows = pl.ds(j * step, step)
        w_copies.append(pltpu.make_async_copy(w_hbm.at[rows], w_vmem.at[rows], sem.at[j]))
        w_copies[-1].start()
    acc = acc_ref[0]
    blocks = tok_ref[...].astype(jnp.float32)
    heads = s0_ref.shape[0]
    hd = s0_ref.shape[2]
    width = heads * hd
    q = blocks[:, 0:width]
    fl = blocks[:, width:2 * width]
    v = blocks[:, 2 * width:3 * width]
    g = blocks[:, 3 * width:4 * width]
    t_len = q.shape[0]
    a = lower_bound + (1.0 - lower_bound) * (1.0 / (1.0 + jnp.exp(-fl)))
    b = 1.0 - a
    la = jnp.log(a)
    row = lax.broadcasted_iota(jnp.int32, (t_len, t_len), 0)
    col = lax.broadcasted_iota(jnp.int32, (t_len, t_len), 1)
    causal = (col <= row).astype(jnp.float32)
    lc = _dot(causal, la)
    big_a = jnp.exp(lc)
    inv_a = jnp.exp(-lc)
    qa = q * big_a
    ba = b * inv_a
    kept_t = (lax.broadcasted_iota(jnp.int32, (la.shape[1], t_len), 1) < acc).astype(jnp.float32)
    a_col = jnp.exp(jnp.sum(kept_t * jnp.transpose(la), axis=1, keepdims=True))
    w_t = kept_t * a_col * jnp.transpose(ba)
    gain = gain_ref[...]
    silu_g = g * (1.0 / (1.0 + jnp.exp(-g)))
    for h in range(heads):
        lanes = slice(h * hd, (h + 1) * hd)
        s0 = s0_ref[h]
        v_h = v[:, lanes]
        qa_h = qa[:, lanes]
        scores = lax.dot_general(qa_h, ba[:, lanes], (((1,), (1,)), ((), ())),
                                 precision=HI, preferred_element_type=jnp.float32)
        o_h = _dot(qa_h, s0) + _dot(scores * causal, v_h)
        new_ref[h] = a_col[lanes] * s0 + _dot(w_t[lanes], v_h)
        meansq = jnp.mean(o_h * o_h, axis=-1, keepdims=True)
        mixed = o_h * lax.rsqrt(meansq + norm_eps) * gain * silu_g[:, lanes]
        mixed_scr[:, lanes] = mixed.astype(mixed_scr.dtype)
    for w_copy in w_copies:
        w_copy.wait()
    chunk = part_ref.shape[2]
    mixed_all = mixed_scr[...]
    for j in range(part_ref.shape[0]):
        part_ref[j] = jnp.dot(mixed_all, w_vmem[:, j * chunk:(j + 1) * chunk],
                              preferred_element_type=jnp.float32)


def mixer(acc, tok, s0, gain, weight, parts):
    heads, hd = s0.shape[0], s0.shape[2]
    t_len = tok.shape[0]
    vmem = pl.BlockSpec(memory_space=pltpu.VMEM)
    return pl.pallas_call(
        mixer_kernel,
        out_shape=(jax.ShapeDtypeStruct(s0.shape, jnp.float32),
                   jax.ShapeDtypeStruct((parts, t_len, weight.shape[1] // parts), jnp.float32)),
        in_specs=[pl.BlockSpec(memory_space=pltpu.SMEM), vmem, vmem, vmem,
                  pl.BlockSpec(memory_space=pl.ANY)],
        out_specs=(vmem, vmem),
        scratch_shapes=[pltpu.VMEM(weight.shape, weight.dtype),
                        pltpu.VMEM((t_len, heads * hd), jnp.bfloat16),
                        pltpu.SemaphoreType.DMA((4,))],
    )(acc, tok, s0, gain, weight)


def route_two_stage(token_tuple, dealing):
    rows, width = token_tuple[0].shape[1:]
    wide = width * len(token_tuple)
    total = wide + 128
    lane = lax.broadcasted_iota(jnp.int32, (rows, total), 1)
    payload = jnp.broadcast_to((dealing[0] + 1).astype(jnp.bfloat16), (rows, total))
    for i, t in enumerate(token_tuple):
        placed = jnp.pad(t[0], ((0, 0), (i * width, total - (i + 1) * width)))
        inside = (lane >= i * width) & (lane < (i + 1) * width)
        payload = jnp.where(inside, placed, payload)
    gathered = lax.all_gather(payload, ROW, axis=0, tiled=False)
    dest = gathered[:, 0, wide].astype(jnp.int32) - 1
    body = gathered[:, :, :wide]
    xn = lax.axis_size("x")
    zh_n = lax.axis_size("zh")
    zl_n = lax.axis_size("zl")
    cn = lax.axis_size("c")
    my_zh = lax.axis_index("zh")
    my_c = lax.axis_index("c")
    xs = jnp.arange(xn, dtype=jnp.int32)[:, None]
    zls = jnp.arange(zl_n, dtype=jnp.int32)[None, :]
    target = (((xs * zh_n + my_zh) * zl_n + zls) * cn + my_c).reshape(-1)
    count = dest.shape[0]
    slots = jnp.arange(count, dtype=jnp.int32)
    idx = jnp.min(jnp.where(target[:, None] == dest[None, :], slots[None, :], count), axis=1)
    send = jnp.take(body, idx, axis=0, mode="fill", fill_value=0)
    send = send.reshape((xn, zl_n) + send.shape[1:])
    got = lax.all_to_all(send, "x", 0, 0, tiled=False)
    part = jnp.sum(got.astype(jnp.float32), axis=0).astype(jnp.bfloat16)
    got = lax.all_to_all(part, "zl", 0, 0, tiled=False)
    return jnp.sum(got.astype(jnp.float32), axis=0).astype(jnp.bfloat16)


def per_device(
    queries,
    forget_logits,
    values,
    gate_input,
    init_states,
    norm_gain,
    out_weight,
    dealing,
    accepted,
):
    local_count = queries.shape[0]
    draft_len = queries.shape[1]
    head_local = init_states.shape[1]
    head_size = init_states.shape[3]
    token_tuple = (queries, forget_logits, values, gate_input)
    got = route_two_stage(token_tuple, dealing)
    hn = lax.axis_size("head")
    new_states, partial_out = mixer(accepted, got, init_states[0], norm_gain.reshape(1, head_size), out_weight, hn)
    new_states = new_states[None]
    swapped = lax.all_to_all(partial_out, "head", 0, 0, tiled=True)
    summed = jnp.sum(swapped, axis=0)
    verified = summed.astype(jnp.bfloat16).reshape(local_count, draft_len, summed.shape[1])
    return (verified, new_states)


def solution(mesh):
    xs, cs, zl = 4, 2, 4
    zh = mesh.shape["req"] // (xs * cs * zl)
    sub = Mesh(mesh.devices.reshape(xs, zh, zl, cs, mesh.shape["head"]), ("x", "zh", "zl", "c", "head"))
    placed = (
        P(REQ, None, "head"),
        P(REQ, None, "head"),
        P(REQ, None, "head"),
        P(REQ, None, "head"),
        P(REQ, "head", None, None),
        P(),
        P("head", None),
        P(REQ),
        P(REQ),
    )
    return jax.shard_map(
        per_device,
        mesh=sub,
        in_specs=placed,
        out_specs=(P(REQ, None, "head"), P(REQ, "head", None, None)),
        check_vma=False,
    )
```

```python
import jax
import jax.numpy as jnp
from jax import lax
from jax.experimental import pallas as pl
from jax.experimental.pallas import tpu as pltpu
from jax.sharding import Mesh, PartitionSpec as P

lower_bound = 0.8
norm_eps = 1e-05

ROW = ("zh", "c")
REQ = ("x", "zh", "zl", "c")


HI = lax.Precision.HIGHEST


def _dot(a, b):
    return jnp.dot(a, b, precision=HI, preferred_element_type=jnp.float32)


def mixer_kernel(acc_ref, tok_ref, s0_ref, gain_ref, w_hbm, new_ref, part_ref, w_vmem, mixed_scr, sem):
    pieces = sem.shape[0]
    step = w_hbm.shape[0] // pieces
    w_copies = []
    for j in range(pieces):
        rows = pl.ds(j * step, step)
        w_copies.append(pltpu.make_async_copy(w_hbm.at[rows], w_vmem.at[rows], sem.at[j]))
        w_copies[-1].start()
    acc = acc_ref[0]
    blocks = tok_ref[...].astype(jnp.float32)
    heads = s0_ref.shape[0]
    hd = s0_ref.shape[2]
    width = heads * hd
    q = blocks[:, 0:width]
    fl = blocks[:, width:2 * width]
    v = blocks[:, 2 * width:3 * width]
    g = blocks[:, 3 * width:4 * width]
    t_len = q.shape[0]
    a = lower_bound + (1.0 - lower_bound) * (1.0 / (1.0 + jnp.exp(-fl)))
    b = 1.0 - a
    la = jnp.log(a)
    row = lax.broadcasted_iota(jnp.int32, (t_len, t_len), 0)
    col = lax.broadcasted_iota(jnp.int32, (t_len, t_len), 1)
    causal = (col <= row).astype(jnp.float32)
    lc = _dot(causal, la)
    big_a = jnp.exp(lc)
    inv_a = jnp.exp(-lc)
    qa = q * big_a
    ba = b * inv_a
    kept_t = (lax.broadcasted_iota(jnp.int32, (la.shape[1], t_len), 1) < acc).astype(jnp.float32)
    a_col = jnp.exp(jnp.sum(kept_t * jnp.transpose(la), axis=1, keepdims=True))
    w_t = kept_t * a_col * jnp.transpose(ba)
    gain = gain_ref[...]
    silu_g = g * (1.0 / (1.0 + jnp.exp(-g)))
    for h in range(heads):
        lanes = slice(h * hd, (h + 1) * hd)
        s0 = s0_ref[h]
        v_h = v[:, lanes]
        qa_h = qa[:, lanes]
        scores = lax.dot_general(qa_h, ba[:, lanes], (((1,), (1,)), ((), ())),
                                 precision=HI, preferred_element_type=jnp.float32)
        o_h = _dot(qa_h, s0) + _dot(scores * causal, v_h)
        new_ref[h] = a_col[lanes] * s0 + _dot(w_t[lanes], v_h)
        meansq = jnp.mean(o_h * o_h, axis=-1, keepdims=True)
        mixed = o_h * lax.rsqrt(meansq + norm_eps) * gain * silu_g[:, lanes]
        mixed_scr[:, lanes] = mixed.astype(mixed_scr.dtype)
    for w_copy in w_copies:
        w_copy.wait()
    chunk = part_ref.shape[2]
    mixed_all = mixed_scr[...]
    for j in range(part_ref.shape[0]):
        part_ref[j] = jnp.dot(mixed_all, w_vmem[:, j * chunk:(j + 1) * chunk],
                              preferred_element_type=jnp.float32)


def mixer(acc, tok, s0, gain, weight, parts):
    heads, hd = s0.shape[0], s0.shape[2]
    t_len = tok.shape[0]
    vmem = pl.BlockSpec(memory_space=pltpu.VMEM)
    return pl.pallas_call(
        mixer_kernel,
        out_shape=(jax.ShapeDtypeStruct(s0.shape, jnp.float32),
                   jax.ShapeDtypeStruct((parts, t_len, weight.shape[1] // parts), jnp.float32)),
        in_specs=[pl.BlockSpec(memory_space=pltpu.SMEM), vmem, vmem, vmem,
                  pl.BlockSpec(memory_space=pl.ANY)],
        out_specs=(vmem, vmem),
        scratch_shapes=[pltpu.VMEM(weight.shape, weight.dtype),
                        pltpu.VMEM((t_len, heads * hd), jnp.bfloat16),
                        pltpu.SemaphoreType.DMA((4,))],
    )(acc, tok, s0, gain, weight)


def route_two_stage(token_tuple, dealing):
    rows, width = token_tuple[0].shape[1:]
    wide = width * len(token_tuple)
    total = wide + 128
    lane = lax.broadcasted_iota(jnp.int32, (rows, total), 1)
    payload = jnp.broadcast_to((dealing[0] + 1).astype(jnp.bfloat16), (rows, total))
    for i, t in enumerate(token_tuple):
        placed = jnp.pad(t[0], ((0, 0), (i * width, total - (i + 1) * width)))
        inside = (lane >= i * width) & (lane < (i + 1) * width)
        payload = jnp.where(inside, placed, payload)
    far = lax.all_gather(payload, "zh", axis=0, tiled=False)
    near = lax.ppermute(far, "c", [(0, 1), (1, 0)])
    gathered = jnp.concatenate([far, near], axis=0)
    dest = gathered[:, 0, wide].astype(jnp.int32) - 1
    body = gathered[:, :, :wide]
    xn = lax.axis_size("x")
    zh_n = lax.axis_size("zh")
    zl_n = lax.axis_size("zl")
    cn = lax.axis_size("c")
    my_zh = lax.axis_index("zh")
    my_c = lax.axis_index("c")
    xs = jnp.arange(xn, dtype=jnp.int32)[:, None]
    zls = jnp.arange(zl_n, dtype=jnp.int32)[None, :]
    target = (((xs * zh_n + my_zh) * zl_n + zls) * cn + my_c).reshape(-1)
    count = dest.shape[0]
    slots = jnp.arange(count, dtype=jnp.int32)
    idx = jnp.min(jnp.where(target[:, None] == dest[None, :], slots[None, :], count), axis=1)
    send = jnp.take(body, idx, axis=0, mode="fill", fill_value=0)
    send = send.reshape((xn, zl_n) + send.shape[1:])
    got = lax.all_to_all(send, "x", 0, 0, tiled=False)
    part = jnp.sum(got.astype(jnp.float32), axis=0).astype(jnp.bfloat16)
    got = lax.all_to_all(part, "zl", 0, 0, tiled=False)
    return jnp.sum(got.astype(jnp.float32), axis=0).astype(jnp.bfloat16)


def per_device(
    queries,
    forget_logits,
    values,
    gate_input,
    init_states,
    norm_gain,
    out_weight,
    dealing,
    accepted,
):
    local_count = queries.shape[0]
    draft_len = queries.shape[1]
    head_local = init_states.shape[1]
    head_size = init_states.shape[3]
    token_tuple = (queries, forget_logits, values, gate_input)
    got = route_two_stage(token_tuple, dealing)
    hn = lax.axis_size("head")
    new_states, partial_out = mixer(accepted, got, init_states[0], norm_gain.reshape(1, head_size), out_weight, hn)
    new_states = new_states[None]
    swapped = lax.all_to_all(partial_out, "head", 0, 0, tiled=True)
    summed = jnp.sum(swapped, axis=0)
    verified = summed.astype(jnp.bfloat16).reshape(local_count, draft_len, summed.shape[1])
    return (verified, new_states)


def solution(mesh):
    xs, cs, zl = 4, 2, 4
    zh = mesh.shape["req"] // (xs * cs * zl)
    sub = Mesh(mesh.devices.reshape(xs, zh, zl, cs, mesh.shape["head"]), ("x", "zh", "zl", "c", "head"))
    placed = (
        P(REQ, None, "head"),
        P(REQ, None, "head"),
        P(REQ, None, "head"),
        P(REQ, None, "head"),
        P(REQ, "head", None, None),
        P(),
        P("head", None),
        P(REQ),
        P(REQ),
    )
    return jax.shard_map(
        per_device,
        mesh=sub,
        in_specs=placed,
        out_specs=(P(REQ, None, "head"), P(REQ, "head", None, None)),
        check_vma=False,
    )
```

```python
import jax
import jax.numpy as jnp
from jax import lax
from jax.experimental import pallas as pl
from jax.experimental.pallas import tpu as pltpu
from jax.sharding import Mesh, PartitionSpec as P

lower_bound = 0.8
norm_eps = 1e-05

ROW = ("c", "zh")
REQ = ("x", "zh", "zl", "c")


HI = lax.Precision.HIGHEST


def _dot(a, b):
    return jnp.dot(a, b, precision=HI, preferred_element_type=jnp.float32)


def mixer_kernel(acc_ref, tok_ref, s0_ref, gain_ref, w_hbm, new_ref, part_ref, w_vmem, mixed_scr, sem):
    pieces = sem.shape[0]
    step = w_hbm.shape[0] // pieces
    w_copies = []
    for j in range(pieces):
        rows = pl.ds(j * step, step)
        w_copies.append(pltpu.make_async_copy(w_hbm.at[rows], w_vmem.at[rows], sem.at[j]))
        w_copies[-1].start()
    acc = acc_ref[0]
    blocks = tok_ref[...].astype(jnp.float32)
    heads = s0_ref.shape[0]
    hd = s0_ref.shape[2]
    width = heads * hd
    q = blocks[:, 0:width]
    fl = blocks[:, width:2 * width]
    v = blocks[:, 2 * width:3 * width]
    g = blocks[:, 3 * width:4 * width]
    t_len = q.shape[0]
    a = lower_bound + (1.0 - lower_bound) * (1.0 / (1.0 + jnp.exp(-fl)))
    b = 1.0 - a
    la = jnp.log(a)
    row = lax.broadcasted_iota(jnp.int32, (t_len, t_len), 0)
    col = lax.broadcasted_iota(jnp.int32, (t_len, t_len), 1)
    causal = (col <= row).astype(jnp.float32)
    lc = _dot(causal, la)
    big_a = jnp.exp(lc)
    inv_a = jnp.exp(-lc)
    qa = q * big_a
    ba = b * inv_a
    kept_t = (lax.broadcasted_iota(jnp.int32, (la.shape[1], t_len), 1) < acc).astype(jnp.float32)
    a_col = jnp.exp(jnp.sum(kept_t * jnp.transpose(la), axis=1, keepdims=True))
    w_t = kept_t * a_col * jnp.transpose(ba)
    gain = gain_ref[...]
    silu_g = g * (1.0 / (1.0 + jnp.exp(-g)))
    for h in range(heads):
        lanes = slice(h * hd, (h + 1) * hd)
        s0 = s0_ref[h]
        v_h = v[:, lanes]
        qa_h = qa[:, lanes]
        scores = lax.dot_general(qa_h, ba[:, lanes], (((1,), (1,)), ((), ())),
                                 precision=HI, preferred_element_type=jnp.float32)
        o_h = _dot(qa_h, s0) + _dot(scores * causal, v_h)
        new_ref[h] = a_col[lanes] * s0 + _dot(w_t[lanes], v_h)
        meansq = jnp.mean(o_h * o_h, axis=-1, keepdims=True)
        mixed = o_h * lax.rsqrt(meansq + norm_eps) * gain * silu_g[:, lanes]
        mixed_scr[:, lanes] = mixed.astype(mixed_scr.dtype)
    for w_copy in w_copies:
        w_copy.wait()
    chunk = part_ref.shape[2]
    mixed_all = mixed_scr[...]
    for j in range(part_ref.shape[0]):
        part_ref[j] = jnp.dot(mixed_all, w_vmem[:, j * chunk:(j + 1) * chunk],
                              preferred_element_type=jnp.float32)


def mixer(acc, tok, s0, gain, weight, parts):
    heads, hd = s0.shape[0], s0.shape[2]
    t_len = tok.shape[0]
    vmem = pl.BlockSpec(memory_space=pltpu.VMEM)
    return pl.pallas_call(
        mixer_kernel,
        out_shape=(jax.ShapeDtypeStruct(s0.shape, jnp.float32),
                   jax.ShapeDtypeStruct((parts, t_len, weight.shape[1] // parts), jnp.float32)),
        in_specs=[pl.BlockSpec(memory_space=pltpu.SMEM), vmem, vmem, vmem,
                  pl.BlockSpec(memory_space=pl.ANY)],
        out_specs=(vmem, vmem),
        scratch_shapes=[pltpu.VMEM(weight.shape, weight.dtype),
                        pltpu.VMEM((t_len, heads * hd), jnp.bfloat16),
                        pltpu.SemaphoreType.DMA((4,))],
    )(acc, tok, s0, gain, weight)


def route_two_stage(token_tuple, dealing):
    rows, width = token_tuple[0].shape[1:]
    wide = width * len(token_tuple)
    total = wide + 128
    lane = lax.broadcasted_iota(jnp.int32, (rows, total), 1)
    payload = jnp.broadcast_to((dealing[0] + 1).astype(jnp.bfloat16), (rows, total))
    for i, t in enumerate(token_tuple):
        placed = jnp.pad(t[0], ((0, 0), (i * width, total - (i + 1) * width)))
        inside = (lane >= i * width) & (lane < (i + 1) * width)
        payload = jnp.where(inside, placed, payload)
    gathered = lax.all_gather(payload, ROW, axis=0, tiled=False)
    dest = gathered[:, 0, wide].astype(jnp.int32) - 1
    body = gathered[:, :, :wide]
    xn = lax.axis_size("x")
    zh_n = lax.axis_size("zh")
    zl_n = lax.axis_size("zl")
    cn = lax.axis_size("c")
    my_zh = lax.axis_index("zh")
    my_c = lax.axis_index("c")
    xs = jnp.arange(xn, dtype=jnp.int32)[:, None]
    zls = jnp.arange(zl_n, dtype=jnp.int32)[None, :]
    target = (((xs * zh_n + my_zh) * zl_n + zls) * cn + my_c).reshape(-1)
    count = dest.shape[0]
    slots = jnp.arange(count, dtype=jnp.int32)
    idx = jnp.min(jnp.where(target[:, None] == dest[None, :], slots[None, :], count), axis=1)
    send = jnp.take(body, idx, axis=0, mode="fill", fill_value=0)
    send = send.reshape((xn, zl_n) + send.shape[1:])
    got = lax.all_to_all(send, "x", 0, 0, tiled=False)
    part = jnp.sum(got.astype(jnp.float32), axis=0).astype(jnp.bfloat16)
    got = lax.all_to_all(part, "zl", 0, 0, tiled=False)
    return jnp.sum(got.astype(jnp.float32), axis=0).astype(jnp.bfloat16)


def per_device(
    queries,
    forget_logits,
    values,
    gate_input,
    init_states,
    norm_gain,
    out_weight,
    dealing,
    accepted,
):
    local_count = queries.shape[0]
    draft_len = queries.shape[1]
    head_local = init_states.shape[1]
    head_size = init_states.shape[3]
    token_tuple = (queries, forget_logits, values, gate_input)
    got = route_two_stage(token_tuple, dealing)
    hn = lax.axis_size("head")
    new_states, partial_out = mixer(accepted, got, init_states[0], norm_gain.reshape(1, head_size), out_weight, hn)
    new_states = new_states[None]
    swapped = lax.all_to_all(partial_out, "head", 0, 0, tiled=True)
    summed = jnp.sum(swapped, axis=0)
    verified = summed.astype(jnp.bfloat16).reshape(local_count, draft_len, summed.shape[1])
    return (verified, new_states)


def solution(mesh):
    xs, cs, zl = 4, 2, 4
    zh = mesh.shape["req"] // (xs * cs * zl)
    sub = Mesh(mesh.devices.reshape(xs, zh, zl, cs, mesh.shape["head"]), ("x", "zh", "zl", "c", "head"))
    placed = (
        P(REQ, None, "head"),
        P(REQ, None, "head"),
        P(REQ, None, "head"),
        P(REQ, None, "head"),
        P(REQ, "head", None, None),
        P(),
        P("head", None),
        P(REQ),
        P(REQ),
    )
    return jax.shard_map(
        per_device,
        mesh=sub,
        in_specs=placed,
        out_specs=(P(REQ, None, "head"), P(REQ, "head", None, None)),
        check_vma=False,
    )
```
